128 devices in a mesh: seq: 32 (over y, x, z_lo), chan: 4 (over z_hi, core).
Axes of the slice: x: 4, y: 4, z: 4 (z_hi: 2, z_lo: 2; z = z_hi * 2 + z_lo), core: 2. Of those that a mesh axis runs over, the one named last changes fastest.
Arguments:
- tokens: bfloat16 [24576, 4096], P('seq', 'chan'), may hold values from -4 to 4
- w_in: bfloat16 [8, 4096, 1296], P('chan', 'seq'), may hold values from -1 to 1
- conv_w: float32 [8, 4, 1280], P('chan'), may hold values from -3 to 3
- conv_b: float32 [8, 1280], P('chan'), may hold values from -3 to 3
- dt_bias: float32 [8, 16], P('chan'), may hold values from -8 to 2
- a_log: float32 [8, 16], P('chan'), may hold values from -4.6 to -3.7
- d_skip: float32 [8, 16], P('chan'), may hold values from 0.3 to 3
- norm_gain: float32 [8, 1024], P('chan'), may hold values from 0.5 to 1.5
Outputs:
- mixer_out: bfloat16 [24576, 8192], P('seq', 'chan')
The draws below stay inside these ranges and needn't reach their ends.
All inputs are finite; a program needn't handle non-finite values.
Results may differ from the reference program's by a relative error of at most 0.0076.
Values may be sent and summed in bfloat16 or wider, within the bound.
No kernel may reach another device: no remote copies, remote signals or barrier semaphores. Data moves between devices by JAX's collectives and lax.ppermute only.
A program may use at most 128 MiB of HBM per device.

```python
import math
import jax
import jax.numpy as jnp
from jax import lax

D = 4096
P_SIZE = 64
N = 128
G = 8
KCONV = 4
Q = 128
HG = 16
GW = 1024
CW = 1280
COLS = 1296
TOKENS = 24576


def sign_pattern(key):
    flips = jax.random.bernoulli(jax.random.fold_in(key, 11), 0.5, (D,))
    return jnp.where(flips, 1.0, -1.0).astype(jnp.float32)


def draw_tokens(key, part):
    base_key = jax.random.fold_in(key, 21)
    drawn_vals = jnp.clip(jax.random.normal(base_key, (TOKENS, D), jnp.float32), -4.0, 4.0)
    spike_at = jax.random.randint(jax.random.fold_in(key, 22), (3,), 0, TOKENS)
    marked = jnp.any(jnp.arange(TOKENS)[:, None] == spike_at[None, :], axis=1)
    spiked = 2.7 * sign_pattern(key)[None, :] + 0.25 * drawn_vals
    return jnp.where(marked[:, None], spiked, drawn_vals).astype(jnp.bfloat16)


def draw_w_in(key, part):
    kernel_key = jax.random.fold_in(key, 31)
    drawn_vals = jnp.clip(jax.random.normal(kernel_key, (G, D, COLS), jnp.float32), -4.0, 4.0)
    drawn_vals = drawn_vals * D ** (-0.5)
    dt_mask = (jnp.arange(COLS) >= CW).astype(jnp.float32)
    extra = 9.0 / D * sign_pattern(key)[None, :, None] * dt_mask[None, None, :]
    return (drawn_vals + extra).astype(jnp.bfloat16)


def draw_dt_bias(key, part):
    fast_share = 0.5
    is_fast = jax.random.bernoulli(jax.random.fold_in(key, 41), fast_share, (G, HG))
    slow_vals = jax.random.uniform(jax.random.fold_in(key, 42), (G, HG), jnp.float32, -8.0, -7.0)
    fast_vals = jax.random.uniform(jax.random.fold_in(key, 43), (G, HG), jnp.float32, 1.0, 2.0)
    return jnp.where(is_fast, fast_vals, slow_vals)


def block_scale(stream_key, shape, pieces, low, top_value):
    def one(position, parts):
        steps = jax.random.uniform(jax.random.fold_in(jax.random.fold_in(stream_key, 6), position), (parts,), jnp.float32, low / len(pieces), top_value / len(pieces))
        return jnp.repeat(jnp.exp(steps), shape[position] // parts).reshape((-1,) + (1,) * (len(shape) - position - 1))

    level = one(*pieces[0])
    for cut in pieces[1:]:
        level = level * one(*cut)
    return level


def noise(own_key, extent, scale, reach, shards=(), held_as=jnp.bfloat16):
    result = scale * jax.random.normal(own_key, extent, jnp.float32)
    if shards:
        result = result * block_scale(own_key, extent, shards, -0.22, 0.18)
    return jnp.clip(result, -reach, reach).astype(held_as)


def setup_inputs(seed: int = 0) -> dict:
    key_of = jax.random.split(jax.random.key(seed), 9)
    return {
        "tokens": draw_tokens(jax.random.fold_in(key_of[8], 71), 0),
        "w_in": draw_w_in(jax.random.fold_in(key_of[8], 71), 0),
        "conv_w": noise(key_of[2], (G, KCONV, CW), 0.5, 3.0, ((0, 4),), jnp.float32),
        "conv_b": noise(key_of[3], (G, CW), 0.3, 3.0, ((0, 4),), jnp.float32),
        "dt_bias": draw_dt_bias(jax.random.fold_in(key_of[8], 71), 0),
        "a_log": jnp.clip(-4.6 + 0.89999986 * jax.random.uniform(key_of[5], (G, HG), jnp.float32) ** block_scale(key_of[5], (G, HG), ((0, 4),), -0.2, 0.2), -4.6, -3.7),
        "d_skip": jnp.clip(jnp.exp(math.log(3.0) - 2.3025851 * jax.random.uniform(key_of[6], (G, HG), jnp.float32) ** block_scale(key_of[6], (G, HG), ((0, 4),), -0.2, 0.2)), 0.3, 3.0),
        "norm_gain": jnp.clip(1.0 + 0.1 * jax.random.normal(key_of[7], (G, GW), jnp.float32), 0.5, 1.5),
    }


epsilon = 1e-05

def one_group(tokens, group_weight, group_kernel, group_shift, group_bias, group_alog, group_skip, group_gain):
    projected = jnp.dot(tokens, group_weight, preferred_element_type=jnp.float32)
    conv_in = projected[:, :CW].astype(jnp.bfloat16)
    raw_dt = projected[:, CW:]
    padded = jnp.concatenate([jnp.zeros((KCONV - 1, CW), jnp.bfloat16), conv_in], axis=0)
    pre_act = jnp.broadcast_to(group_shift[None, :], (TOKENS, CW))
    for offset in range(KCONV):
        pre_act = pre_act + group_kernel[offset][None, :] * padded[offset:offset + TOKENS]
    inputs = jax.nn.silu(pre_act).astype(jnp.bfloat16)
    block_count = TOKENS // Q
    x_all = inputs[:, :GW].reshape(block_count, Q, HG, P_SIZE)
    b_all = inputs[:, GW:GW + N].reshape(block_count, Q, N)
    c_all = inputs[:, GW + N:].reshape(block_count, Q, N)
    step_dt = jax.nn.softplus(raw_dt + group_bias[None, :]).reshape(block_count, Q, HG)
    decay_rate = -jnp.exp(group_alog)
    cumulative = jnp.cumsum(decay_rate[None, None, :] * step_dt, axis=1)
    causal = lax.broadcasted_iota(jnp.int32, (Q, Q), 0) >= lax.broadcasted_iota(jnp.int32, (Q, Q), 1)

    def per_block(state_now, block_in):
        x_blk, b_blk, c_blk, dt_blk, cum_blk = block_in
        scores = jnp.dot(c_blk, b_blk.T, preferred_element_type=jnp.float32)
        cum_cols = cum_blk.T
        dt_cols = dt_blk.T
        spread = cum_cols[:, :, None] - cum_cols[:, None, :]
        damping = jnp.where(causal[None], jnp.exp(jnp.minimum(spread, 0.0)), 0.0)
        weights = lax.optimization_barrier((scores[None] * damping * dt_cols[:, None, :]).astype(jnp.bfloat16)).astype(jnp.float32)
        inner = jnp.einsum('hij,jhp->ihp', weights, x_blk.astype(jnp.float32))
        rounded_state = lax.optimization_barrier(state_now.astype(jnp.bfloat16)).astype(jnp.float32)
        across = jnp.einsum('in,hpn->ihp', c_blk.astype(jnp.float32), rounded_state)
        activity = inner + jnp.exp(cum_blk)[:, :, None] * across + group_skip[None, :, None] * x_blk
        last_cum = cum_blk[-1]
        tail_factor = jnp.exp(last_cum[None, :] - cum_blk) * dt_blk
        scaled = lax.optimization_barrier((x_blk * tail_factor[:, :, None]).astype(jnp.bfloat16)).astype(jnp.float32)
        fresh_state = jnp.einsum('jhp,jn->hpn', scaled, b_blk.astype(jnp.float32))
        return (jnp.exp(last_cum)[:, None, None] * state_now + fresh_state, activity)
    zero_state = jnp.zeros((HG, P_SIZE, N), jnp.float32)
    _, activity = lax.scan(per_block, zero_state, (x_all, b_all, c_all, step_dt, cumulative))
    flat_act = activity.reshape(TOKENS, GW)
    inv_rms = lax.rsqrt(lax.optimization_barrier(jnp.mean(flat_act * flat_act, axis=-1, keepdims=True)) + epsilon)
    return (flat_act * inv_rms * group_gain[None, :]).astype(jnp.bfloat16)

def reference(tokens, w_in, conv_w, conv_b, dt_bias, a_log, d_skip, norm_gain):

    def group_entry(group_args):
        return one_group(tokens, group_args[0], group_args[1], group_args[2], group_args[3], group_args[4], group_args[5], group_args[6])
    outputs = lax.map(group_entry, (w_in, conv_w, conv_b, dt_bias, a_log, d_skip, norm_gain))
    return jnp.transpose(outputs, (1, 0, 2)).reshape(TOKENS, G * GW)
```

```python
import jax
import jax.numpy as jnp
from jax import lax
from jax.sharding import PartitionSpec as P

P_SIZE = 64
N = 128
KCONV = 4
Q = 128
HG = 16
GW = 1024
CW = 1280


epsilon = 1e-05


def shifted(block, axis, distance):
    devices = range(lax.axis_size(axis))
    route = [(i - distance, i) for i in devices if i - distance in devices]
    return lax.ppermute(block, axis, route)


def entering(keep, end, axis):
    place = lax.axis_index(axis)
    size = lax.axis_size(axis)
    keep = jnp.where(place == 0, 1.0, shifted(keep, axis, 1))
    end = shifted(end, axis, 1)
    distance = 1
    while distance < size:
        earlier_end = shifted(end, axis, distance)
        reach = place >= distance
        end = jnp.where(reach, keep[..., None, None] * earlier_end + end, end)
        if distance * 2 < size:
            earlier_keep = shifted(keep, axis, distance)
            keep = jnp.where(reach, keep * earlier_keep, keep)
        distance *= 2
    return end


def mix_groups(gathered, w_in, conv_w, conv_b, dt_bias, a_log, d_skip, norm_gain):
    groups = w_in.shape[0]
    row_count = gathered.shape[0]
    rows_first = jnp.transpose(w_in, (1, 0, 2))
    full_w = lax.all_gather(rows_first, "seq", axis=0, tiled=True)
    projected = jnp.einsum(
        "td,dgc->tgc",
        gathered,
        full_w,
        preferred_element_type=jnp.float32,
    )
    conv_in = projected[:, :, :CW].astype(jnp.bfloat16)
    raw_dt = projected[:, :, CW:]
    rim_rows = shifted(conv_in[row_count - (KCONV - 1) :], "seq", 1)
    padded = jnp.concatenate([rim_rows, conv_in], axis=0)
    pre_act = jnp.broadcast_to(conv_b[None], (row_count, groups, CW))
    for offset in range(KCONV):
        pre_act = pre_act + conv_w[None, :, offset] * padded[offset : offset + row_count]
    inputs = jax.nn.silu(pre_act).astype(jnp.bfloat16)
    block_count = row_count // Q
    blocked = inputs.reshape(block_count, Q, groups, CW)
    x_all = blocked[..., :GW].reshape(block_count, Q, groups, HG, P_SIZE)
    b_all = blocked[..., GW : GW + N]
    c_all = blocked[..., GW + N :]
    step_dt = jax.nn.softplus(raw_dt + dt_bias[None]).reshape(block_count, Q, groups, HG)
    decay_rate = -jnp.exp(a_log)
    cumulative = jnp.cumsum(decay_rate[None, None] * step_dt, axis=1)
    causal = lax.broadcasted_iota(jnp.int32, (Q, Q), 0) >= lax.broadcasted_iota(
        jnp.int32, (Q, Q), 1
    )

    last_cum = cumulative[:, -1]
    keep_all = jnp.exp(last_cum)
    tail_factor = jnp.exp(last_cum[:, None] - cumulative) * step_dt
    scaled = (x_all * tail_factor[..., None]).astype(jnp.bfloat16)
    fresh_all = jnp.einsum(
        "qjghp,qjgn->qghpn", scaled, b_all, preferred_element_type=jnp.float32
    )

    local_states = []
    state_now = jnp.zeros(fresh_all.shape[1:], jnp.float32)
    keep_now = jnp.ones(keep_all.shape[1:], jnp.float32)
    keep_before = []
    for q in range(block_count):
        local_states.append(state_now)
        keep_before.append(keep_now)
        state_now = keep_all[q][..., None, None] * state_now + fresh_all[q]
        keep_now = keep_now * keep_all[q]
    incoming = entering(keep_now, state_now, "seq")
    states = jnp.stack(local_states) + jnp.stack(keep_before)[..., None, None] * incoming[None]

    scores = jnp.einsum("qign,qjgn->qgij", c_all, b_all, preferred_element_type=jnp.float32)
    cum_cols = jnp.transpose(cumulative, (0, 2, 3, 1))
    dt_cols = jnp.transpose(step_dt, (0, 2, 3, 1))
    spread = cum_cols[..., :, None] - cum_cols[..., None, :]
    damping = jnp.where(causal, jnp.exp(jnp.minimum(spread, 0.0)), 0.0)
    weights = (scores[:, :, None] * damping * dt_cols[..., None, :]).astype(jnp.bfloat16)
    partial_y = jnp.einsum(
        "qghij,qjghp->qighp", weights, x_all, preferred_element_type=jnp.float32
    )
    partial_y = partial_y + d_skip[None, None, :, :, None] * x_all

    across = jnp.einsum(
        "qign,qghpn->qighp",
        c_all,
        states.astype(jnp.bfloat16),
        preferred_element_type=jnp.float32,
    )
    activity = partial_y + jnp.exp(cumulative)[..., None] * across
    flat_act = activity.reshape(row_count, groups, GW)
    inv_rms = lax.rsqrt(jnp.mean(flat_act * flat_act, axis=-1, keepdims=True) + epsilon)
    normed = (flat_act * inv_rms * norm_gain[None]).astype(jnp.bfloat16)
    return normed.reshape(row_count, groups * GW)


def per_device(tokens, w_in, conv_w, conv_b, dt_bias, a_log, d_skip, norm_gain):
    gathered = lax.all_gather(tokens, "chan", axis=1, tiled=True)
    return mix_groups(gathered, w_in, conv_w, conv_b, dt_bias, a_log, d_skip, norm_gain)


def solution(mesh):
    return jax.shard_map(
        per_device,
        mesh=mesh,
        in_specs=(
            P("seq", "chan"),
            P("chan", "seq", None),
            P("chan", None, None),
            P("chan", None),
            P("chan", None),
            P("chan", None),
            P("chan", None),
            P("chan", None),
        ),
        out_specs=P("seq", "chan"),
        check_vma=False,
    )
```

```python
import jax
import jax.numpy as jnp
from jax import lax
from jax.sharding import Mesh, PartitionSpec as P

P_SIZE = 64
N = 128
KCONV = 4
Q = 128
HG = 16
GW = 1024
CW = 1280


epsilon = 1e-05
SEQ = "seq"


def shifted(block, axis, distance):
    devices = range(lax.axis_size(axis))
    route = [(i - distance, i) for i in devices if i - distance in devices]
    return lax.ppermute(block, axis, route)


def entering(keep, end, axis):
    place = lax.axis_index(axis)
    size = lax.axis_size(axis)
    keep = jnp.where(place == 0, 1.0, shifted(keep, axis, 1))
    end = shifted(end, axis, 1)
    distance = 1
    while distance < size:
        earlier_end = shifted(end, axis, distance)
        reach = place >= distance
        end = jnp.where(reach, keep[..., None, None] * earlier_end + end, end)
        if distance * 2 < size:
            earlier_keep = shifted(keep, axis, distance)
            keep = jnp.where(reach, keep * earlier_keep, keep)
        distance *= 2
    return end


def mix_groups(gathered, w_in, conv_w, conv_b, dt_bias, a_log, d_skip, norm_gain):
    groups = w_in.shape[0]
    row_count = gathered.shape[0]
    rows_first = jnp.transpose(w_in, (1, 0, 2))
    if isinstance(SEQ, tuple):
        pair_w = lax.all_gather(rows_first, SEQ[2], axis=0, tiled=True)
        full_w = lax.all_gather(pair_w, SEQ[:2], axis=0, tiled=True)
    else:
        full_w = lax.all_gather(rows_first, SEQ, axis=0, tiled=True)
    projected = jnp.einsum(
        "td,dgc->tgc",
        gathered,
        full_w,
        preferred_element_type=jnp.float32,
    )
    conv_in = projected[:, :, :CW].astype(jnp.bfloat16)
    raw_dt = projected[:, :, CW:]
    rim_rows = shifted(conv_in[row_count - (KCONV - 1) :], SEQ, 1)
    padded = jnp.concatenate([rim_rows, conv_in], axis=0)
    pre_act = jnp.broadcast_to(conv_b[None], (row_count, groups, CW))
    for offset in range(KCONV):
        pre_act = pre_act + conv_w[None, :, offset] * padded[offset : offset + row_count]
    inputs = jax.nn.silu(pre_act).astype(jnp.bfloat16)
    block_count = row_count // Q
    blocked = inputs.reshape(block_count, Q, groups, CW)
    x_all = blocked[..., :GW].reshape(block_count, Q, groups, HG, P_SIZE)
    b_all = blocked[..., GW : GW + N]
    c_all = blocked[..., GW + N :]
    step_dt = jax.nn.softplus(raw_dt + dt_bias[None]).reshape(block_count, Q, groups, HG)
    decay_rate = -jnp.exp(a_log)
    cumulative = jnp.cumsum(decay_rate[None, None] * step_dt, axis=1)
    causal = lax.broadcasted_iota(jnp.int32, (Q, Q), 0) >= lax.broadcasted_iota(
        jnp.int32, (Q, Q), 1
    )

    last_cum = cumulative[:, -1]
    keep_all = jnp.exp(last_cum)
    tail_factor = jnp.exp(last_cum[:, None] - cumulative) * step_dt
    scaled = (x_all * tail_factor[..., None]).astype(jnp.bfloat16)
    fresh_all = jnp.einsum(
        "qjghp,qjgn->qghpn", scaled, b_all, preferred_element_type=jnp.float32
    )

    local_states = []
    state_now = jnp.zeros(fresh_all.shape[1:], jnp.float32)
    keep_now = jnp.ones(keep_all.shape[1:], jnp.float32)
    keep_before = []
    for q in range(block_count):
        local_states.append(state_now)
        keep_before.append(keep_now)
        state_now = keep_all[q][..., None, None] * state_now + fresh_all[q]
        keep_now = keep_now * keep_all[q]
    incoming = entering(keep_now, state_now, SEQ)
    states = jnp.stack(local_states) + jnp.stack(keep_before)[..., None, None] * incoming[None]

    scores = jnp.einsum("qign,qjgn->qgij", c_all, b_all, preferred_element_type=jnp.float32)
    cum_cols = jnp.transpose(cumulative, (0, 2, 3, 1))
    dt_cols = jnp.transpose(step_dt, (0, 2, 3, 1))
    spread = cum_cols[..., :, None] - cum_cols[..., None, :]
    damping = jnp.where(causal, jnp.exp(jnp.minimum(spread, 0.0)), 0.0)
    weights = (scores[:, :, None] * damping * dt_cols[..., None, :]).astype(jnp.bfloat16)
    partial_y = jnp.einsum(
        "qghij,qjghp->qighp", weights, x_all, preferred_element_type=jnp.float32
    )
    partial_y = partial_y + d_skip[None, None, :, :, None] * x_all

    across = jnp.einsum(
        "qign,qghpn->qighp",
        c_all,
        states.astype(jnp.bfloat16),
        preferred_element_type=jnp.float32,
    )
    activity = partial_y + jnp.exp(cumulative)[..., None] * across
    flat_act = activity.reshape(row_count, groups, GW)
    inv_rms = lax.rsqrt(jnp.mean(flat_act * flat_act, axis=-1, keepdims=True) + epsilon)
    normed = (flat_act * inv_rms * norm_gain[None]).astype(jnp.bfloat16)
    return normed.reshape(row_count, groups * GW)


def per_device(tokens, w_in, conv_w, conv_b, dt_bias, a_log, d_skip, norm_gain):
    gathered = lax.all_gather(tokens, "chan", axis=1, tiled=True)
    return mix_groups(gathered, w_in, conv_w, conv_b, dt_bias, a_log, d_skip, norm_gain)


def split_mesh(mesh):
    global SEQ
    devices = mesh.devices
    try:
        flat = devices.reshape(-1)
        across_y = len({d.coords[1] for d in flat})
        across_x = len({d.coords[0] for d in flat})
    except (AttributeError, IndexError, TypeError):
        SEQ = "seq"
        return mesh
    seq_size, chan_size = devices.shape
    if seq_size % (across_y * across_x) or across_y * across_x == seq_size:
        SEQ = "seq"
        return mesh
    pair = seq_size // (across_y * across_x)
    SEQ = ("y", "x", "zl")
    return Mesh(devices.reshape(across_y, across_x, pair, chan_size), SEQ + ("chan",))


def solution(mesh):
    mesh = split_mesh(mesh)
    return jax.shard_map(
        per_device,
        mesh=mesh,
        in_specs=(
            P(SEQ, "chan"),
            P("chan", SEQ, None),
            P("chan", None, None),
            P("chan", None),
            P("chan", None),
            P("chan", None),
            P("chan", None),
            P("chan", None),
        ),
        out_specs=P(SEQ, "chan"),
        check_vma=False,
    )
```

```python
import jax
import jax.numpy as jnp
from jax import lax
from jax.sharding import Mesh, PartitionSpec as P

P_SIZE = 64
N = 128
KCONV = 4
Q = 128
HG = 16
GW = 1024
CW = 1280


epsilon = 1e-05
SEQ = "seq"


def shifted(block, axis, distance):
    devices = range(lax.axis_size(axis))
    route = [(i - distance, i) for i in devices if i - distance in devices]
    return lax.ppermute(block, axis, route)


def combine(earlier, later):
    return (earlier[0] * later[0], later[0][..., None, None] * earlier[1] + later[1])


def gather_level(own, axis, need_total):
    size = lax.axis_size(axis)
    place = lax.axis_index(axis)
    groups, heads = own[0].shape
    tail = own[1].shape[-1]
    packed = jnp.concatenate(
        [own[1], jnp.broadcast_to(own[0][..., None, None], (groups, heads, 8, tail))], axis=2
    )
    received = [None]
    for distance in range(1, size):
        if need_total:
            route = [(i, (i + distance) % size) for i in range(size)]
        else:
            route = [(i, i + distance) for i in range(size - distance)]
        got = lax.ppermute(packed, axis, route)
        received.append((got[:, :, -8, 0], got[:, :, :-8]))
    prefix = (jnp.ones_like(own[0]), jnp.zeros_like(own[1]))
    for distance in range(size - 1, 0, -1):
        joined = combine(prefix, received[distance])
        reach = distance <= place
        prefix = (jnp.where(reach, joined[0], prefix[0]), jnp.where(reach, joined[1], prefix[1]))
    if not need_total:
        return prefix, None
    total = combine(prefix, own)
    for distance in range(size - 1, 0, -1):
        joined = combine(total, received[distance])
        beyond = distance > place
        total = (jnp.where(beyond, joined[0], total[0]), jnp.where(beyond, joined[1], total[1]))
    return prefix, total


def entering(keep, end, axes):
    carried = (keep, end)
    prefixes = []
    for level, axis in enumerate(reversed(axes)):
        prefix, carried = gather_level(carried, axis, level < len(axes) - 1)
        prefixes.append(prefix)
    result = prefixes[-1]
    for prefix in reversed(prefixes[:-1]):
        result = combine(result, prefix)
    return result[1]


def mix_groups(gathered, w_in, conv_w, conv_b, dt_bias, a_log, d_skip, norm_gain):
    groups = w_in.shape[0]
    row_count = gathered.shape[0]
    rows_first = jnp.transpose(w_in, (1, 0, 2))
    if isinstance(SEQ, tuple):
        pair_w = lax.all_gather(rows_first, SEQ[2], axis=0, tiled=True)
        full_w = lax.all_gather(pair_w, SEQ[:2], axis=0, tiled=True)
    else:
        full_w = lax.all_gather(rows_first, SEQ, axis=0, tiled=True)
    projected = jnp.einsum(
        "td,dgc->tgc",
        gathered,
        full_w,
        preferred_element_type=jnp.float32,
    )
    conv_in = projected[:, :, :CW].astype(jnp.bfloat16)
    raw_dt = projected[:, :, CW:]
    rim_rows = shifted(conv_in[row_count - (KCONV - 1) :], SEQ, 1)
    padded = jnp.concatenate([rim_rows, conv_in], axis=0)
    pre_act = jnp.broadcast_to(conv_b[None], (row_count, groups, CW))
    for offset in range(KCONV):
        pre_act = pre_act + conv_w[None, :, offset] * padded[offset : offset + row_count]
    inputs = jax.nn.silu(pre_act).astype(jnp.bfloat16)
    block_count = row_count // Q
    blocked = inputs.reshape(block_count, Q, groups, CW)
    x_all = blocked[..., :GW].reshape(block_count, Q, groups, HG, P_SIZE)
    b_all = blocked[..., GW : GW + N]
    c_all = blocked[..., GW + N :]
    step_dt = jax.nn.softplus(raw_dt + dt_bias[None]).reshape(block_count, Q, groups, HG)
    decay_rate = -jnp.exp(a_log)
    cumulative = jnp.cumsum(decay_rate[None, None] * step_dt, axis=1)
    causal = lax.broadcasted_iota(jnp.int32, (Q, Q), 0) >= lax.broadcasted_iota(
        jnp.int32, (Q, Q), 1
    )

    last_cum = cumulative[:, -1]
    keep_all = jnp.exp(last_cum)
    tail_factor = jnp.exp(last_cum[:, None] - cumulative) * step_dt
    scaled = (x_all * tail_factor[..., None]).astype(jnp.bfloat16)
    fresh_all = jnp.einsum(
        "qjghp,qjgn->qghpn", scaled, b_all, preferred_element_type=jnp.float32
    )

    local_states = []
    state_now = jnp.zeros(fresh_all.shape[1:], jnp.float32)
    keep_now = jnp.ones(keep_all.shape[1:], jnp.float32)
    keep_before = []
    for q in range(block_count):
        local_states.append(state_now)
        keep_before.append(keep_now)
        state_now = keep_all[q][..., None, None] * state_now + fresh_all[q]
        keep_now = keep_now * keep_all[q]
    incoming = entering(keep_now, state_now, SEQ if isinstance(SEQ, tuple) else (SEQ,))
    states = jnp.stack(local_states) + jnp.stack(keep_before)[..., None, None] * incoming[None]

    scores = jnp.einsum("qign,qjgn->qgij", c_all, b_all, preferred_element_type=jnp.float32)
    cum_cols = jnp.transpose(cumulative, (0, 2, 3, 1))
    dt_cols = jnp.transpose(step_dt, (0, 2, 3, 1))
    spread = cum_cols[..., :, None] - cum_cols[..., None, :]
    damping = jnp.where(causal, jnp.exp(jnp.minimum(spread, 0.0)), 0.0)
    weights = (scores[:, :, None] * damping * dt_cols[..., None, :]).astype(jnp.bfloat16)
    partial_y = jnp.einsum(
        "qghij,qjghp->qighp", weights, x_all, preferred_element_type=jnp.float32
    )
    partial_y = partial_y + d_skip[None, None, :, :, None] * x_all

    across = jnp.einsum(
        "qign,qghpn->qighp",
        c_all,
        states.astype(jnp.bfloat16),
        preferred_element_type=jnp.float32,
    )
    activity = partial_y + jnp.exp(cumulative)[..., None] * across
    flat_act = activity.reshape(row_count, groups, GW)
    inv_rms = lax.rsqrt(jnp.mean(flat_act * flat_act, axis=-1, keepdims=True) + epsilon)
    normed = (flat_act * inv_rms * norm_gain[None]).astype(jnp.bfloat16)
    return normed.reshape(row_count, groups * GW)


def per_device(tokens, w_in, conv_w, conv_b, dt_bias, a_log, d_skip, norm_gain):
    gathered = lax.all_gather(tokens, "chan", axis=1, tiled=True)
    return mix_groups(gathered, w_in, conv_w, conv_b, dt_bias, a_log, d_skip, norm_gain)


def split_mesh(mesh):
    global SEQ
    devices = mesh.devices
    try:
        flat = devices.reshape(-1)
        across_y = len({d.coords[1] for d in flat})
        across_x = len({d.coords[0] for d in flat})
    except (AttributeError, IndexError, TypeError):
        SEQ = "seq"
        return mesh
    seq_size, chan_size = devices.shape
    if seq_size % (across_y * across_x) or across_y * across_x == seq_size:
        SEQ = "seq"
        return mesh
    pair = seq_size // (across_y * across_x)
    SEQ = ("y", "x", "zl")
    return Mesh(devices.reshape(across_y, across_x, pair, chan_size), SEQ + ("chan",))


def solution(mesh):
    mesh = split_mesh(mesh)
    return jax.shard_map(
        per_device,
        mesh=mesh,
        in_specs=(
            P(SEQ, "chan"),
            P("chan", SEQ, None),
            P("chan", None, None),
            P("chan", None),
            P("chan", None),
            P("chan", None),
            P("chan", None),
            P("chan", None),
        ),
        out_specs=P(SEQ, "chan"),
        check_vma=False,
    )
```

```python
import jax
import jax.numpy as jnp
from jax import lax
from jax.sharding import Mesh, PartitionSpec as P

P_SIZE = 64
N = 128
KCONV = 4
Q = 128
HG = 16
GW = 1024
CW = 1280


epsilon = 1e-05
SEQ = "seq"


def shifted(block, axis, distance):
    devices = range(lax.axis_size(axis))
    route = [(i - distance, i) for i in devices if i - distance in devices]
    return lax.ppermute(block, axis, route)


def combine(earlier, later):
    return (earlier[0] * later[0], later[0][..., None, None] * earlier[1] + later[1])


def gather_level(own, axis, need_total):
    size = lax.axis_size(axis)
    place = lax.axis_index(axis)
    groups, heads = own[0].shape
    tail = own[1].shape[-1]
    packed = jnp.concatenate(
        [own[1], jnp.broadcast_to(own[0][..., None, None], (groups, heads, 8, tail))], axis=2
    )
    received = [None]
    for distance in range(1, size):
        if need_total:
            route = [(i, (i + distance) % size) for i in range(size)]
        else:
            route = [(i, i + distance) for i in range(size - distance)]
        got = lax.ppermute(packed, axis, route)
        received.append((got[:, :, -8, 0], got[:, :, :-8]))
    prefix = (jnp.ones_like(own[0]), jnp.zeros_like(own[1]))
    for distance in range(size - 1, 0, -1):
        joined = combine(prefix, received[distance])
        reach = distance <= place
        prefix = (jnp.where(reach, joined[0], prefix[0]), jnp.where(reach, joined[1], prefix[1]))
    if not need_total:
        return prefix, None
    total = combine(prefix, own)
    for distance in range(size - 1, 0, -1):
        joined = combine(total, received[distance])
        beyond = distance > place
        total = (jnp.where(beyond, joined[0], total[0]), jnp.where(beyond, joined[1], total[1]))
    return prefix, total


def entering(keep, end, axes):
    carried = (keep, end)
    prefixes = []
    for level, axis in enumerate(reversed(axes)):
        prefix, carried = gather_level(carried, axis, level < len(axes) - 1)
        prefixes.append(prefix)
    result = prefixes[-1]
    for prefix in reversed(prefixes[:-1]):
        result = combine(result, prefix)
    return result[1]


def mix_groups(gathered, w_in, conv_w, conv_b, dt_bias, a_log, d_skip, norm_gain):
    groups = w_in.shape[0]
    row_count = gathered.shape[0]
    rows_first = jnp.transpose(w_in, (1, 0, 2))
    if isinstance(SEQ, tuple):
        pair_w = lax.all_gather(rows_first, SEQ[2], axis=0, tiled=True)
        full_w = lax.all_gather(pair_w, SEQ[:2], axis=0, tiled=True)
    else:
        full_w = lax.all_gather(rows_first, SEQ, axis=0, tiled=True)
    projected = jnp.einsum(
        "td,dgc->tgc",
        gathered,
        full_w,
        preferred_element_type=jnp.float32,
    )
    conv_in = projected[:, :, :CW].astype(jnp.bfloat16)
    raw_dt = projected[:, :, CW:]
    rim_rows = shifted(conv_in[row_count - (KCONV - 1) :], SEQ, 1)
    padded = jnp.concatenate([rim_rows, conv_in], axis=0)
    pre_act = jnp.broadcast_to(conv_b[None], (row_count, groups, CW))
    for offset in range(KCONV):
        pre_act = pre_act + conv_w[None, :, offset] * padded[offset : offset + row_count]
    inputs = jax.nn.silu(pre_act).astype(jnp.bfloat16)
    block_count = row_count // Q
    blocked = inputs.reshape(block_count, Q, groups, CW)
    x_all = blocked[..., :GW].reshape(block_count, Q, groups, HG, P_SIZE)
    b_all = blocked[..., GW : GW + N]
    c_all = blocked[..., GW + N :]
    step_dt = jax.nn.softplus(raw_dt + dt_bias[None]).reshape(block_count, Q, groups, HG)
    decay_rate = -jnp.exp(a_log)
    cumulative = jnp.cumsum(decay_rate[None, None] * step_dt, axis=1)
    causal = lax.broadcasted_iota(jnp.int32, (Q, Q), 0) >= lax.broadcasted_iota(
        jnp.int32, (Q, Q), 1
    )

    last_cum = cumulative[:, -1]
    keep_all = jnp.exp(last_cum)
    tail_factor = jnp.exp(last_cum[:, None] - cumulative) * step_dt
    scaled = (x_all * tail_factor[..., None]).astype(jnp.bfloat16)
    fresh_all = jnp.einsum(
        "qjghp,qjgn->qghpn", scaled, b_all, preferred_element_type=jnp.float32
    )

    local_states = []
    state_now = jnp.zeros(fresh_all.shape[1:], jnp.float32)
    keep_now = jnp.ones(keep_all.shape[1:], jnp.float32)
    keep_before = []
    for q in range(block_count):
        local_states.append(state_now)
        keep_before.append(keep_now)
        state_now = keep_all[q][..., None, None] * state_now + fresh_all[q]
        keep_now = keep_now * keep_all[q]
    incoming = entering(keep_now, state_now, SEQ if isinstance(SEQ, tuple) else (SEQ,))
    states = jnp.stack(local_states) + jnp.stack(keep_before)[..., None, None] * incoming[None]

    scores = jnp.einsum("qign,qjgn->qgij", c_all, b_all, preferred_element_type=jnp.float32)
    cum_cols = jnp.transpose(cumulative, (0, 2, 3, 1))
    dt_cols = jnp.transpose(step_dt, (0, 2, 3, 1))
    spread = cum_cols[..., :, None] - cum_cols[..., None, :]
    damping = jnp.where(causal, jnp.exp(jnp.minimum(spread, 0.0)), 0.0)
    weights = (scores[:, :, None] * damping * dt_cols[..., None, :]).astype(jnp.bfloat16)
    partial_y = jnp.einsum(
        "qghij,qjghp->qighp", weights, x_all, preferred_element_type=jnp.float32
    )
    partial_y = partial_y + d_skip[None, None, :, :, None] * x_all

    across = jnp.einsum(
        "qign,qghpn->qighp",
        c_all,
        states.astype(jnp.bfloat16),
        preferred_element_type=jnp.float32,
    )
    activity = partial_y + jnp.exp(cumulative)[..., None] * across
    flat_act = activity.reshape(row_count, groups, GW)
    inv_rms = lax.rsqrt(jnp.mean(flat_act * flat_act, axis=-1, keepdims=True) + epsilon)
    normed = (flat_act * inv_rms * norm_gain[None]).astype(jnp.bfloat16)
    return normed.reshape(row_count, groups * GW)


def per_device(tokens, w_in, conv_w, conv_b, dt_bias, a_log, d_skip, norm_gain):
    size = lax.axis_size("chan")
    place = lax.axis_index("chan")
    width = tokens.shape[1]
    gathered = jnp.zeros((tokens.shape[0], width * size), tokens.dtype)
    for distance in range(size):
        if distance:
            piece = lax.ppermute(
                tokens, "chan", [(i, (i + distance) % size) for i in range(size)]
            )
        else:
            piece = tokens
        source = (place - distance) % size
        gathered = lax.dynamic_update_slice(gathered, piece, (0, source * width))
    return mix_groups(gathered, w_in, conv_w, conv_b, dt_bias, a_log, d_skip, norm_gain)


def split_mesh(mesh):
    global SEQ
    devices = mesh.devices
    try:
        flat = devices.reshape(-1)
        across_y = len({d.coords[1] for d in flat})
        across_x = len({d.coords[0] for d in flat})
    except (AttributeError, IndexError, TypeError):
        SEQ = "seq"
        return mesh
    seq_size, chan_size = devices.shape
    if seq_size % (across_y * across_x) or across_y * across_x == seq_size:
        SEQ = "seq"
        return mesh
    pair = seq_size // (across_y * across_x)
    SEQ = ("y", "x", "zl")
    return Mesh(devices.reshape(across_y, across_x, pair, chan_size), SEQ + ("chan",))


def solution(mesh):
    mesh = split_mesh(mesh)
    return jax.shard_map(
        per_device,
        mesh=mesh,
        in_specs=(
            P(SEQ, "chan"),
            P("chan", SEQ, None),
            P("chan", None, None),
            P("chan", None),
            P("chan", None),
            P("chan", None),
            P("chan", None),
            P("chan", None),
        ),
        out_specs=P(SEQ, "chan"),
        check_vma=False,
    )
```

```python
import jax
import jax.numpy as jnp
from jax import lax
from jax.sharding import Mesh, PartitionSpec as P

P_SIZE = 64
N = 128
KCONV = 4
Q = 128
HG = 16
GW = 1024
CW = 1280


epsilon = 1e-05
SEQ = "seq"


def shifted(block, axis, distance):
    devices = range(lax.axis_size(axis))
    route = [(i - distance, i) for i in devices if i - distance in devices]
    return lax.ppermute(block, axis, route)


def combine(earlier, later):
    return (earlier[0] * later[0], later[0][..., None, None] * earlier[1] + later[1])


def gather_level(own, axis, need_total):
    size = lax.axis_size(axis)
    place = lax.axis_index(axis)
    groups, heads = own[0].shape
    tail = own[1].shape[-1]
    packed = jnp.concatenate(
        [own[1], jnp.broadcast_to(own[0][..., None, None], (groups, heads, 8, tail))], axis=2
    )
    received = [None]
    for distance in range(1, size):
        if need_total:
            route = [(i, (i + distance) % size) for i in range(size)]
        else:
            route = [(i, i + distance) for i in range(size - distance)]
        got = lax.ppermute(packed, axis, route)
        received.append((got[:, :, -8, 0], got[:, :, :-8]))
    prefix = (jnp.ones_like(own[0]), jnp.zeros_like(own[1]))
    for distance in range(size - 1, 0, -1):
        joined = combine(prefix, received[distance])
        reach = distance <= place
        prefix = (jnp.where(reach, joined[0], prefix[0]), jnp.where(reach, joined[1], prefix[1]))
    if not need_total:
        return prefix, None
    total = combine(prefix, own)
    for distance in range(size - 1, 0, -1):
        joined = combine(total, received[distance])
        beyond = distance > place
        total = (jnp.where(beyond, joined[0], total[0]), jnp.where(beyond, joined[1], total[1]))
    return prefix, total


def entering(keep, end, axes):
    carried = (keep, end)
    prefixes = []
    for level, axis in enumerate(reversed(axes)):
        prefix, carried = gather_level(carried, axis, level < len(axes) - 1)
        prefixes.append(prefix)
    result = prefixes[-1]
    for prefix in reversed(prefixes[:-1]):
        result = combine(result, prefix)
    return result[1]


def mix_groups(gathered, w_in, conv_w, conv_b, dt_bias, a_log, d_skip, norm_gain):
    groups = w_in.shape[0]
    row_count = gathered.shape[0]
    rows_first = jnp.transpose(w_in, (1, 0, 2))
    if isinstance(SEQ, tuple):
        pair = lax.axis_size(SEQ[2])
        slot = lax.axis_index(SEQ[2])
        piece = rows_first.shape[0]
        pair_w = jnp.zeros((piece * pair,) + rows_first.shape[1:], rows_first.dtype)
        for distance in range(pair):
            if distance:
                rows = lax.ppermute(
                    rows_first, SEQ[2], [(i, (i + distance) % pair) for i in range(pair)]
                )
            else:
                rows = rows_first
            source = (slot - distance) % pair
            pair_w = lax.dynamic_update_slice(pair_w, rows, (source * piece, 0, 0))
        full_w = lax.all_gather(pair_w, SEQ[:2], axis=0, tiled=True)
    else:
        full_w = lax.all_gather(rows_first, SEQ, axis=0, tiled=True)
    projected = jnp.einsum(
        "td,dgc->tgc",
        gathered,
        full_w,
        preferred_element_type=jnp.float32,
    )
    conv_in = projected[:, :, :CW].astype(jnp.bfloat16)
    raw_dt = projected[:, :, CW:]
    rim_rows = shifted(conv_in[row_count - (KCONV - 1) :], SEQ, 1)
    padded = jnp.concatenate([rim_rows, conv_in], axis=0)
    pre_act = jnp.broadcast_to(conv_b[None], (row_count, groups, CW))
    for offset in range(KCONV):
        pre_act = pre_act + conv_w[None, :, offset] * padded[offset : offset + row_count]
    inputs = jax.nn.silu(pre_act).astype(jnp.bfloat16)
    block_count = row_count // Q
    blocked = inputs.reshape(block_count, Q, groups, CW)
    x_all = blocked[..., :GW].reshape(block_count, Q, groups, HG, P_SIZE)
    b_all = blocked[..., GW : GW + N]
    c_all = blocked[..., GW + N :]
    step_dt = jax.nn.softplus(raw_dt + dt_bias[None]).reshape(block_count, Q, groups, HG)
    decay_rate = -jnp.exp(a_log)
    cumulative = jnp.cumsum(decay_rate[None, None] * step_dt, axis=1)
    causal = lax.broadcasted_iota(jnp.int32, (Q, Q), 0) >= lax.broadcasted_iota(
        jnp.int32, (Q, Q), 1
    )

    last_cum = cumulative[:, -1]
    keep_all = jnp.exp(last_cum)
    tail_factor = jnp.exp(last_cum[:, None] - cumulative) * step_dt
    scaled = (x_all * tail_factor[..., None]).astype(jnp.bfloat16)
    fresh_all = jnp.einsum(
        "qjghp,qjgn->qghpn", scaled, b_all, preferred_element_type=jnp.float32
    )

    local_states = []
    state_now = jnp.zeros(fresh_all.shape[1:], jnp.float32)
    keep_now = jnp.ones(keep_all.shape[1:], jnp.float32)
    keep_before = []
    for q in range(block_count):
        local_states.append(state_now)
        keep_before.append(keep_now)
        state_now = keep_all[q][..., None, None] * state_now + fresh_all[q]
        keep_now = keep_now * keep_all[q]
    incoming = entering(keep_now, state_now, SEQ if isinstance(SEQ, tuple) else (SEQ,))
    states = jnp.stack(local_states) + jnp.stack(keep_before)[..., None, None] * incoming[None]

    scores = jnp.einsum("qign,qjgn->qgij", c_all, b_all, preferred_element_type=jnp.float32)
    cum_cols = jnp.transpose(cumulative, (0, 2, 3, 1))
    dt_cols = jnp.transpose(step_dt, (0, 2, 3, 1))
    spread = cum_cols[..., :, None] - cum_cols[..., None, :]
    damping = jnp.where(causal, jnp.exp(jnp.minimum(spread, 0.0)), 0.0)
    weights = (scores[:, :, None] * damping * dt_cols[..., None, :]).astype(jnp.bfloat16)
    partial_y = jnp.einsum(
        "qghij,qjghp->qighp", weights, x_all, preferred_element_type=jnp.float32
    )
    partial_y = partial_y + d_skip[None, None, :, :, None] * x_all

    across = jnp.einsum(
        "qign,qghpn->qighp",
        c_all,
        states.astype(jnp.bfloat16),
        preferred_element_type=jnp.float32,
    )
    activity = partial_y + jnp.exp(cumulative)[..., None] * across
    flat_act = activity.reshape(row_count, groups, GW)
    inv_rms = lax.rsqrt(jnp.mean(flat_act * flat_act, axis=-1, keepdims=True) + epsilon)
    normed = (flat_act * inv_rms * norm_gain[None]).astype(jnp.bfloat16)
    return normed.reshape(row_count, groups * GW)


def per_device(tokens, w_in, conv_w, conv_b, dt_bias, a_log, d_skip, norm_gain):
    size = lax.axis_size("chan")
    place = lax.axis_index("chan")
    width = tokens.shape[1]
    gathered = jnp.zeros((tokens.shape[0], width * size), tokens.dtype)
    for distance in range(size):
        if distance:
            piece = lax.ppermute(
                tokens, "chan", [(i, (i + distance) % size) for i in range(size)]
            )
        else:
            piece = tokens
        source = (place - distance) % size
        gathered = lax.dynamic_update_slice(gathered, piece, (0, source * width))
    return mix_groups(gathered, w_in, conv_w, conv_b, dt_bias, a_log, d_skip, norm_gain)


def split_mesh(mesh):
    global SEQ
    devices = mesh.devices
    try:
        flat = devices.reshape(-1)
        across_y = len({d.coords[1] for d in flat})
        across_x = len({d.coords[0] for d in flat})
    except (AttributeError, IndexError, TypeError):
        SEQ = "seq"
        return mesh
    seq_size, chan_size = devices.shape
    if seq_size % (across_y * across_x) or across_y * across_x == seq_size:
        SEQ = "seq"
        return mesh
    pair = seq_size // (across_y * across_x)
    SEQ = ("y", "x", "zl")
    return Mesh(devices.reshape(across_y, across_x, pair, chan_size), SEQ + ("chan",))


def solution(mesh):
    mesh = split_mesh(mesh)
    return jax.shard_map(
        per_device,
        mesh=mesh,
        in_specs=(
            P(SEQ, "chan"),
            P("chan", SEQ, None),
            P("chan", None, None),
            P("chan", None),
            P("chan", None),
            P("chan", None),
            P("chan", None),
            P("chan", None),
        ),
        out_specs=P(SEQ, "chan"),
        check_vma=False,
    )
```

```python
import jax
import jax.numpy as jnp
from jax import lax
from jax.sharding import Mesh, PartitionSpec as P

P_SIZE = 64
N = 128
KCONV = 4
Q = 128
HG = 16
GW = 1024
CW = 1280


epsilon = 1e-05
SEQ = "seq"


def shifted(block, axis, distance):
    devices = range(lax.axis_size(axis))
    route = [(i - distance, i) for i in devices if i - distance in devices]
    return lax.ppermute(block, axis, route)


def combine(earlier, later):
    return (earlier[0] * later[0], later[0][..., None, None] * earlier[1] + later[1])


def gather_level(own, axis, need_total):
    size = lax.axis_size(axis)
    place = lax.axis_index(axis)
    groups, heads = own[0].shape
    tail = own[1].shape[-1]
    packed = jnp.concatenate(
        [own[1], jnp.broadcast_to(own[0][..., None, None], (groups, heads, 8, tail))], axis=2
    )
    received = [None]
    for distance in range(1, size):
        if need_total:
            route = [(i, (i + distance) % size) for i in range(size)]
        else:
            route = [(i, i + distance) for i in range(size - distance)]
        got = lax.ppermute(packed, axis, route)
        received.append((got[:, :, -8, 0], got[:, :, :-8]))
    prefix = (jnp.ones_like(own[0]), jnp.zeros_like(own[1]))
    for distance in range(size - 1, 0, -1):
        joined = combine(prefix, received[distance])
        reach = distance <= place
        prefix = (jnp.where(reach, joined[0], prefix[0]), jnp.where(reach, joined[1], prefix[1]))
    if not need_total:
        return prefix, None
    total = combine(prefix, own)
    for distance in range(size - 1, 0, -1):
        joined = combine(total, received[distance])
        beyond = distance > place
        total = (jnp.where(beyond, joined[0], total[0]), jnp.where(beyond, joined[1], total[1]))
    return prefix, total


def entering(keep, end, axes):
    carried = (keep, end)
    prefixes = []
    for level, axis in enumerate(reversed(axes)):
        prefix, carried = gather_level(carried, axis, level < len(axes) - 1)
        prefixes.append(prefix)
    result = prefixes[-1]
    for prefix in reversed(prefixes[:-1]):
        result = combine(result, prefix)
    return result[1]


def mix_groups(gathered, w_in, conv_w, conv_b, dt_bias, a_log, d_skip, norm_gain, after):
    groups = w_in.shape[0]
    row_count = gathered.shape[0]
    rows_first = jnp.transpose(w_in, (1, 0, 2))
    if isinstance(SEQ, tuple):
        pair = lax.axis_size(SEQ[2])
        slot = lax.axis_index(SEQ[2])
        piece = rows_first.shape[0]
        pair_w = jnp.zeros((piece * pair,) + rows_first.shape[1:], rows_first.dtype)
        for distance in range(pair):
            if distance:
                rows = lax.ppermute(
                    rows_first, SEQ[2], [(i, (i + distance) % pair) for i in range(pair)]
                )
            else:
                rows = rows_first
            source = (slot - distance) % pair
            pair_w = lax.dynamic_update_slice(pair_w, rows, (source * piece, 0, 0))
        full_w = lax.all_gather(pair_w, SEQ[:2], axis=0, tiled=True)
    else:
        full_w = lax.all_gather(rows_first, SEQ, axis=0, tiled=True)
    if after is not None:
        full_w, _ = lax.optimization_barrier((full_w, after))
    projected = jnp.einsum(
        "td,dgc->tgc",
        gathered,
        full_w,
        preferred_element_type=jnp.float32,
    )
    conv_in = projected[:, :, :CW].astype(jnp.bfloat16)
    raw_dt = projected[:, :, CW:]
    rim_rows = shifted(conv_in[row_count - (KCONV - 1) :], SEQ, 1)
    padded = jnp.concatenate([rim_rows, conv_in], axis=0)
    pre_act = jnp.broadcast_to(conv_b[None], (row_count, groups, CW))
    for offset in range(KCONV):
        pre_act = pre_act + conv_w[None, :, offset] * padded[offset : offset + row_count]
    inputs = jax.nn.silu(pre_act).astype(jnp.bfloat16)
    block_count = row_count // Q
    blocked = inputs.reshape(block_count, Q, groups, CW)
    x_all = blocked[..., :GW].reshape(block_count, Q, groups, HG, P_SIZE)
    b_all = blocked[..., GW : GW + N]
    c_all = blocked[..., GW + N :]
    step_dt = jax.nn.softplus(raw_dt + dt_bias[None]).reshape(block_count, Q, groups, HG)
    decay_rate = -jnp.exp(a_log)
    cumulative = jnp.cumsum(decay_rate[None, None] * step_dt, axis=1)
    causal = lax.broadcasted_iota(jnp.int32, (Q, Q), 0) >= lax.broadcasted_iota(
        jnp.int32, (Q, Q), 1
    )

    last_cum = cumulative[:, -1]
    keep_all = jnp.exp(last_cum)
    tail_factor = jnp.exp(last_cum[:, None] - cumulative) * step_dt
    scaled = (x_all * tail_factor[..., None]).astype(jnp.bfloat16)
    fresh_all = jnp.einsum(
        "qjghp,qjgn->qghpn", scaled, b_all, preferred_element_type=jnp.float32
    )

    local_states = []
    state_now = jnp.zeros(fresh_all.shape[1:], jnp.float32)
    keep_now = jnp.ones(keep_all.shape[1:], jnp.float32)
    keep_before = []
    for q in range(block_count):
        local_states.append(state_now)
        keep_before.append(keep_now)
        state_now = keep_all[q][..., None, None] * state_now + fresh_all[q]
        keep_now = keep_now * keep_all[q]
    incoming = entering(keep_now, state_now, SEQ if isinstance(SEQ, tuple) else (SEQ,))
    states = jnp.stack(local_states) + jnp.stack(keep_before)[..., None, None] * incoming[None]

    scores = jnp.einsum("qign,qjgn->qgij", c_all, b_all, preferred_element_type=jnp.float32)
    cum_cols = jnp.transpose(cumulative, (0, 2, 3, 1))
    dt_cols = jnp.transpose(step_dt, (0, 2, 3, 1))
    spread = cum_cols[..., :, None] - cum_cols[..., None, :]
    damping = jnp.where(causal, jnp.exp(jnp.minimum(spread, 0.0)), 0.0)
    weights = (scores[:, :, None] * damping * dt_cols[..., None, :]).astype(jnp.bfloat16)
    partial_y = jnp.einsum(
        "qghij,qjghp->qighp", weights, x_all, preferred_element_type=jnp.float32
    )
    partial_y = partial_y + d_skip[None, None, :, :, None] * x_all

    across = jnp.einsum(
        "qign,qghpn->qighp",
        c_all,
        states.astype(jnp.bfloat16),
        preferred_element_type=jnp.float32,
    )
    activity = partial_y + jnp.exp(cumulative)[..., None] * across
    flat_act = activity.reshape(row_count, groups, GW)
    inv_rms = lax.rsqrt(jnp.mean(flat_act * flat_act, axis=-1, keepdims=True) + epsilon)
    normed = (flat_act * inv_rms * norm_gain[None]).astype(jnp.bfloat16)
    return normed.reshape(row_count, groups * GW), state_now


def per_device(tokens, w_in, conv_w, conv_b, dt_bias, a_log, d_skip, norm_gain):
    size = lax.axis_size("chan")
    place = lax.axis_index("chan")
    width = tokens.shape[1]
    gathered = jnp.zeros((tokens.shape[0], width * size), tokens.dtype)
    for distance in range(size):
        if distance:
            piece = lax.ppermute(
                tokens, "chan", [(i, (i + distance) % size) for i in range(size)]
            )
        else:
            piece = tokens
        source = (place - distance) % size
        gathered = lax.dynamic_update_slice(gathered, piece, (0, source * width))
    outputs = []
    after = None
    for g in range(w_in.shape[0]):
        one = slice(g, g + 1)
        normed, after = mix_groups(
            gathered, w_in[one], conv_w[one], conv_b[one], dt_bias[one],
            a_log[one], d_skip[one], norm_gain[one], after,
        )
        outputs.append(normed)
    return jnp.concatenate(outputs, axis=1)


def split_mesh(mesh):
    global SEQ
    devices = mesh.devices
    try:
        flat = devices.reshape(-1)
        across_y = len({d.coords[1] for d in flat})
        across_x = len({d.coords[0] for d in flat})
    except (AttributeError, IndexError, TypeError):
        SEQ = "seq"
        return mesh
    seq_size, chan_size = devices.shape
    if seq_size % (across_y * across_x) or across_y * across_x == seq_size:
        SEQ = "seq"
        return mesh
    pair = seq_size // (across_y * across_x)
    SEQ = ("y", "x", "zl")
    return Mesh(devices.reshape(across_y, across_x, pair, chan_size), SEQ + ("chan",))


def solution(mesh):
    mesh = split_mesh(mesh)
    return jax.shard_map(
        per_device,
        mesh=mesh,
        in_specs=(
            P(SEQ, "chan"),
            P("chan", SEQ, None),
            P("chan", None, None),
            P("chan", None),
            P("chan", None),
            P("chan", None),
            P("chan", None),
            P("chan", None),
        ),
        out_specs=P(SEQ, "chan"),
        check_vma=False,
    )
```

```python
import jax
import jax.numpy as jnp
from jax import lax
from jax.sharding import Mesh, PartitionSpec as P

P_SIZE = 64
N = 128
KCONV = 4
Q = 128
HG = 16
GW = 1024
CW = 1280


epsilon = 1e-05
SEQ = "seq"


def shifted(block, axis, distance):
    devices = range(lax.axis_size(axis))
    route = [(i - distance, i) for i in devices if i - distance in devices]
    return lax.ppermute(block, axis, route)


def combine(earlier, later):
    return (earlier[0] * later[0], later[0][..., None, None] * earlier[1] + later[1])


def gather_level(own, axis, need_total):
    size = lax.axis_size(axis)
    place = lax.axis_index(axis)
    groups, heads = own[0].shape
    shape = own[1].shape
    tail = shape[-1]
    rows = own[1].reshape(groups, -1, tail)
    keep_rows = jnp.pad(own[0][:, None, :], ((0, 0), (0, 7), (0, tail - heads)))
    packed = jnp.concatenate([rows, keep_rows], axis=1)
    body = rows.shape[1]
    received = [None]
    for distance in range(1, size):
        if need_total:
            route = [(i, (i + distance) % size) for i in range(size)]
        else:
            route = [(i, i + distance) for i in range(size - distance)]
        got = lax.ppermute(packed, axis, route)
        received.append((got[:, body, :heads], got[:, :body].reshape(shape)))
    prefix = (jnp.ones_like(own[0]), jnp.zeros_like(own[1]))
    for distance in range(size - 1, 0, -1):
        joined = combine(prefix, received[distance])
        reach = distance <= place
        prefix = (jnp.where(reach, joined[0], prefix[0]), jnp.where(reach, joined[1], prefix[1]))
    if not need_total:
        return prefix, None
    total = combine(prefix, own)
    for distance in range(size - 1, 0, -1):
        joined = combine(total, received[distance])
        beyond = distance > place
        total = (jnp.where(beyond, joined[0], total[0]), jnp.where(beyond, joined[1], total[1]))
    return prefix, total


def entering(keep, end, axes):
    carried = (keep, end)
    prefixes = []
    for level, axis in enumerate(reversed(axes)):
        prefix, carried = gather_level(carried, axis, level < len(axes) - 1)
        prefixes.append(prefix)
    result = prefixes[-1]
    for prefix in reversed(prefixes[:-1]):
        result = combine(result, prefix)
    return result[1]


def mix_groups(gathered, w_in, conv_w, conv_b, dt_bias, a_log, d_skip, norm_gain, after):
    groups = w_in.shape[0]
    row_count = gathered.shape[0]
    rows_first = jnp.transpose(w_in, (1, 0, 2))
    if isinstance(SEQ, tuple):
        pair = lax.axis_size(SEQ[2])
        slot = lax.axis_index(SEQ[2])
        piece = rows_first.shape[0]
        pair_w = jnp.zeros((piece * pair,) + rows_first.shape[1:], rows_first.dtype)
        for distance in range(pair):
            if distance:
                rows = lax.ppermute(
                    rows_first, SEQ[2], [(i, (i + distance) % pair) for i in range(pair)]
                )
            else:
                rows = rows_first
            source = (slot - distance) % pair
            pair_w = lax.dynamic_update_slice(pair_w, rows, (source * piece, 0, 0))
        full_w = lax.all_gather(pair_w, SEQ[:2], axis=0, tiled=True)
    else:
        full_w = lax.all_gather(rows_first, SEQ, axis=0, tiled=True)
    if after is not None:
        full_w, _ = lax.optimization_barrier((full_w, after))
    projected = jnp.einsum(
        "td,dgc->tgc",
        gathered,
        full_w,
        preferred_element_type=jnp.float32,
    )
    conv_in = projected[:, :, :CW].astype(jnp.bfloat16)
    raw_dt = projected[:, :, CW:]
    rim_rows = shifted(conv_in[row_count - (KCONV - 1) :], SEQ, 1)
    padded = jnp.concatenate([rim_rows, conv_in], axis=0)
    pre_act = jnp.broadcast_to(conv_b[None], (row_count, groups, CW))
    for offset in range(KCONV):
        pre_act = pre_act + conv_w[None, :, offset] * padded[offset : offset + row_count]
    inputs = jax.nn.silu(pre_act).astype(jnp.bfloat16)
    block_count = row_count // Q
    blocked = inputs.reshape(block_count, Q, groups, CW)
    x_all = blocked[..., :GW].reshape(block_count, Q, groups, HG, P_SIZE)
    b_all = blocked[..., GW : GW + N]
    c_all = blocked[..., GW + N :]
    step_dt = jax.nn.softplus(raw_dt + dt_bias[None]).reshape(block_count, Q, groups, HG)
    decay_rate = -jnp.exp(a_log)
    cumulative = jnp.cumsum(decay_rate[None, None] * step_dt, axis=1)
    causal = lax.broadcasted_iota(jnp.int32, (Q, Q), 0) >= lax.broadcasted_iota(
        jnp.int32, (Q, Q), 1
    )

    last_cum = cumulative[:, -1]
    keep_all = jnp.exp(last_cum)
    tail_factor = jnp.exp(last_cum[:, None] - cumulative) * step_dt
    scaled = (x_all * tail_factor[..., None]).astype(jnp.bfloat16)
    fresh_all = jnp.einsum(
        "qjghp,qjgn->qghpn", scaled, b_all, preferred_element_type=jnp.float32
    )

    local_states = []
    state_now = jnp.zeros(fresh_all.shape[1:], jnp.float32)
    keep_now = jnp.ones(keep_all.shape[1:], jnp.float32)
    keep_before = []
    for q in range(block_count):
        local_states.append(state_now)
        keep_before.append(keep_now)
        state_now = keep_all[q][..., None, None] * state_now + fresh_all[q]
        keep_now = keep_now * keep_all[q]
    incoming = entering(keep_now, state_now, SEQ if isinstance(SEQ, tuple) else (SEQ,))
    states = jnp.stack(local_states) + jnp.stack(keep_before)[..., None, None] * incoming[None]

    scores = jnp.einsum("qign,qjgn->qgij", c_all, b_all, preferred_element_type=jnp.float32)
    cum_cols = jnp.transpose(cumulative, (0, 2, 3, 1))
    dt_cols = jnp.transpose(step_dt, (0, 2, 3, 1))
    spread = cum_cols[..., :, None] - cum_cols[..., None, :]
    damping = jnp.where(causal, jnp.exp(jnp.minimum(spread, 0.0)), 0.0)
    weights = (scores[:, :, None] * damping * dt_cols[..., None, :]).astype(jnp.bfloat16)
    partial_y = jnp.einsum(
        "qghij,qjghp->qighp", weights, x_all, preferred_element_type=jnp.float32
    )
    partial_y = partial_y + d_skip[None, None, :, :, None] * x_all

    across = jnp.einsum(
        "qign,qghpn->qighp",
        c_all,
        states.astype(jnp.bfloat16),
        preferred_element_type=jnp.float32,
    )
    activity = partial_y + jnp.exp(cumulative)[..., None] * across
    flat_act = activity.reshape(row_count, groups, GW)
    inv_rms = lax.rsqrt(jnp.mean(flat_act * flat_act, axis=-1, keepdims=True) + epsilon)
    normed = (flat_act * inv_rms * norm_gain[None]).astype(jnp.bfloat16)
    return normed.reshape(row_count, groups * GW), state_now


def per_device(tokens, w_in, conv_w, conv_b, dt_bias, a_log, d_skip, norm_gain):
    size = lax.axis_size("chan")
    place = lax.axis_index("chan")
    width = tokens.shape[1]
    gathered = jnp.zeros((tokens.shape[0], width * size), tokens.dtype)
    for distance in range(size):
        if distance:
            piece = lax.ppermute(
                tokens, "chan", [(i, (i + distance) % size) for i in range(size)]
            )
        else:
            piece = tokens
        source = (place - distance) % size
        gathered = lax.dynamic_update_slice(gathered, piece, (0, source * width))
    outputs = []
    after = None
    for g in range(w_in.shape[0]):
        one = slice(g, g + 1)
        normed, after = mix_groups(
            gathered, w_in[one], conv_w[one], conv_b[one], dt_bias[one],
            a_log[one], d_skip[one], norm_gain[one], after,
        )
        outputs.append(normed)
    return jnp.concatenate(outputs, axis=1)


def split_mesh(mesh):
    global SEQ
    devices = mesh.devices
    try:
        flat = devices.reshape(-1)
        across_y = len({d.coords[1] for d in flat})
        across_x = len({d.coords[0] for d in flat})
    except (AttributeError, IndexError, TypeError):
        SEQ = "seq"
        return mesh
    seq_size, chan_size = devices.shape
    if seq_size % (across_y * across_x) or across_y * across_x == seq_size:
        SEQ = "seq"
        return mesh
    pair = seq_size // (across_y * across_x)
    SEQ = ("y", "x", "zl")
    return Mesh(devices.reshape(across_y, across_x, pair, chan_size), SEQ + ("chan",))


def solution(mesh):
    mesh = split_mesh(mesh)
    return jax.shard_map(
        per_device,
        mesh=mesh,
        in_specs=(
            P(SEQ, "chan"),
            P("chan", SEQ, None),
            P("chan", None, None),
            P("chan", None),
            P("chan", None),
            P("chan", None),
            P("chan", None),
            P("chan", None),
        ),
        out_specs=P(SEQ, "chan"),
        check_vma=False,
    )
```

```python
import jax
import jax.numpy as jnp
from jax import lax
from jax.sharding import Mesh, PartitionSpec as P

P_SIZE = 64
N = 128
KCONV = 4
Q = 128
HG = 16
GW = 1024
CW = 1280


epsilon = 1e-05
SEQ = "seq"


def shifted(block, axis, distance):
    devices = range(lax.axis_size(axis))
    route = [(i - distance, i) for i in devices if i - distance in devices]
    return lax.ppermute(block, axis, route)


def combine(earlier, later):
    return (earlier[0] * later[0], later[0][..., None, None] * earlier[1] + later[1])


def gather_level(own, axis, need_total):
    size = lax.axis_size(axis)
    place = lax.axis_index(axis)
    groups, heads = own[0].shape
    shape = own[1].shape
    tail = shape[-1]
    rows = own[1].reshape(groups, -1, tail)
    keep_rows = jnp.pad(own[0][:, None, :], ((0, 0), (0, 7), (0, tail - heads)))
    packed = jnp.concatenate([rows, keep_rows], axis=1)
    body = rows.shape[1]
    received = [None]
    for distance in range(1, size):
        if need_total:
            route = [(i, (i + distance) % size) for i in range(size)]
        else:
            route = [(i, i + distance) for i in range(size - distance)]
        got = lax.ppermute(packed, axis, route)
        received.append((got[:, body, :heads], got[:, :body].reshape(shape)))
    prefix = (jnp.ones_like(own[0]), jnp.zeros_like(own[1]))
    for distance in range(size - 1, 0, -1):
        joined = combine(prefix, received[distance])
        reach = distance <= place
        prefix = (jnp.where(reach, joined[0], prefix[0]), jnp.where(reach, joined[1], prefix[1]))
    if not need_total:
        return prefix, None
    total = combine(prefix, own)
    for distance in range(size - 1, 0, -1):
        joined = combine(total, received[distance])
        beyond = distance > place
        total = (jnp.where(beyond, joined[0], total[0]), jnp.where(beyond, joined[1], total[1]))
    return prefix, total


def entering(keep, end, axes):
    carried = (keep, end)
    prefixes = []
    for level, axis in enumerate(reversed(axes)):
        prefix, carried = gather_level(carried, axis, level < len(axes) - 1)
        prefixes.append(prefix)
    result = prefixes[-1]
    for prefix in reversed(prefixes[:-1]):
        result = combine(result, prefix)
    return result[1]


def mix_groups(gathered, w_in, conv_w, conv_b, dt_bias, a_log, d_skip, norm_gain, after):
    groups = w_in.shape[0]
    row_count = gathered.shape[0]
    rows_first = jnp.transpose(w_in, (1, 0, 2))
    if isinstance(SEQ, tuple):
        pair = lax.axis_size(SEQ[2])
        slot = lax.axis_index(SEQ[2])
        piece = rows_first.shape[0]
        pair_w = jnp.zeros((piece * pair,) + rows_first.shape[1:], rows_first.dtype)
        for distance in range(pair):
            if distance:
                rows = lax.ppermute(
                    rows_first, SEQ[2], [(i, (i + distance) % pair) for i in range(pair)]
                )
            else:
                rows = rows_first
            source = (slot - distance) % pair
            pair_w = lax.dynamic_update_slice(pair_w, rows, (source * piece, 0, 0))
        full_w = lax.all_gather(pair_w, SEQ[:2], axis=0, tiled=True)
    else:
        full_w = lax.all_gather(rows_first, SEQ, axis=0, tiled=True)
    if after is not None:
        link = (after.reshape(-1)[0] * 0).astype(full_w.dtype)
        full_w = full_w.at[0, 0, 0].add(link)
    projected = jnp.einsum(
        "td,dgc->tgc",
        gathered,
        full_w,
        preferred_element_type=jnp.float32,
    )
    conv_in = projected[:, :, :CW].astype(jnp.bfloat16)
    raw_dt = projected[:, :, CW:]
    rim_rows = shifted(conv_in[row_count - (KCONV - 1) :], SEQ, 1)
    padded = jnp.concatenate([rim_rows, conv_in], axis=0)
    pre_act = jnp.broadcast_to(conv_b[None], (row_count, groups, CW))
    for offset in range(KCONV):
        pre_act = pre_act + conv_w[None, :, offset] * padded[offset : offset + row_count]
    inputs = jax.nn.silu(pre_act).astype(jnp.bfloat16)
    block_count = row_count // Q
    blocked = inputs.reshape(block_count, Q, groups, CW)
    x_all = blocked[..., :GW].reshape(block_count, Q, groups, HG, P_SIZE)
    b_all = blocked[..., GW : GW + N]
    c_all = blocked[..., GW + N :]
    step_dt = jax.nn.softplus(raw_dt + dt_bias[None]).reshape(block_count, Q, groups, HG)
    decay_rate = -jnp.exp(a_log)
    cumulative = jnp.cumsum(decay_rate[None, None] * step_dt, axis=1)
    causal = lax.broadcasted_iota(jnp.int32, (Q, Q), 0) >= lax.broadcasted_iota(
        jnp.int32, (Q, Q), 1
    )

    last_cum = cumulative[:, -1]
    keep_all = jnp.exp(last_cum)
    tail_factor = jnp.exp(last_cum[:, None] - cumulative) * step_dt
    scaled = (x_all * tail_factor[..., None]).astype(jnp.bfloat16)
    fresh_all = jnp.einsum(
        "qjghp,qjgn->qghpn", scaled, b_all, preferred_element_type=jnp.float32
    )

    local_states = []
    state_now = jnp.zeros(fresh_all.shape[1:], jnp.float32)
    keep_now = jnp.ones(keep_all.shape[1:], jnp.float32)
    keep_before = []
    for q in range(block_count):
        local_states.append(state_now)
        keep_before.append(keep_now)
        state_now = keep_all[q][..., None, None] * state_now + fresh_all[q]
        keep_now = keep_now * keep_all[q]
    incoming = entering(keep_now, state_now, SEQ if isinstance(SEQ, tuple) else (SEQ,))
    states = jnp.stack(local_states) + jnp.stack(keep_before)[..., None, None] * incoming[None]

    scores = jnp.einsum("qign,qjgn->qgij", c_all, b_all, preferred_element_type=jnp.float32)
    cum_cols = jnp.transpose(cumulative, (0, 2, 3, 1))
    dt_cols = jnp.transpose(step_dt, (0, 2, 3, 1))
    spread = cum_cols[..., :, None] - cum_cols[..., None, :]
    damping = jnp.where(causal, jnp.exp(jnp.minimum(spread, 0.0)), 0.0)
    weights = (scores[:, :, None] * damping * dt_cols[..., None, :]).astype(jnp.bfloat16)
    partial_y = jnp.einsum(
        "qghij,qjghp->qighp", weights, x_all, preferred_element_type=jnp.float32
    )
    partial_y = partial_y + d_skip[None, None, :, :, None] * x_all

    across = jnp.einsum(
        "qign,qghpn->qighp",
        c_all,
        states.astype(jnp.bfloat16),
        preferred_element_type=jnp.float32,
    )
    activity = partial_y + jnp.exp(cumulative)[..., None] * across
    flat_act = activity.reshape(row_count, groups, GW)
    inv_rms = lax.rsqrt(jnp.mean(flat_act * flat_act, axis=-1, keepdims=True) + epsilon)
    normed = (flat_act * inv_rms * norm_gain[None]).astype(jnp.bfloat16)
    return normed.reshape(row_count, groups * GW), incoming


def per_device(tokens, w_in, conv_w, conv_b, dt_bias, a_log, d_skip, norm_gain):
    size = lax.axis_size("chan")
    place = lax.axis_index("chan")
    width = tokens.shape[1]
    gathered = jnp.zeros((tokens.shape[0], width * size), tokens.dtype)
    for distance in range(size):
        if distance:
            piece = lax.ppermute(
                tokens, "chan", [(i, (i + distance) % size) for i in range(size)]
            )
        else:
            piece = tokens
        source = (place - distance) % size
        gathered = lax.dynamic_update_slice(gathered, piece, (0, source * width))
    outputs = []
    after = None
    for g in range(w_in.shape[0]):
        one = slice(g, g + 1)
        normed, after = mix_groups(
            gathered, w_in[one], conv_w[one], conv_b[one], dt_bias[one],
            a_log[one], d_skip[one], norm_gain[one], after,
        )
        outputs.append(normed)
    return jnp.concatenate(outputs, axis=1)


def split_mesh(mesh):
    global SEQ
    devices = mesh.devices
    try:
        flat = devices.reshape(-1)
        across_y = len({d.coords[1] for d in flat})
        across_x = len({d.coords[0] for d in flat})
    except (AttributeError, IndexError, TypeError):
        SEQ = "seq"
        return mesh
    seq_size, chan_size = devices.shape
    if seq_size % (across_y * across_x) or across_y * across_x == seq_size:
        SEQ = "seq"
        return mesh
    pair = seq_size // (across_y * across_x)
    SEQ = ("y", "x", "zl")
    return Mesh(devices.reshape(across_y, across_x, pair, chan_size), SEQ + ("chan",))


def solution(mesh):
    mesh = split_mesh(mesh)
    return jax.shard_map(
        per_device,
        mesh=mesh,
        in_specs=(
            P(SEQ, "chan"),
            P("chan", SEQ, None),
            P("chan", None, None),
            P("chan", None),
            P("chan", None),
            P("chan", None),
            P("chan", None),
            P("chan", None),
        ),
        out_specs=P(SEQ, "chan"),
        check_vma=False,
    )
```

```python
import jax
import jax.numpy as jnp
from jax import lax
from jax.sharding import Mesh, PartitionSpec as P

P_SIZE = 64
N = 128
KCONV = 4
Q = 128
HG = 16
GW = 1024
CW = 1280


epsilon = 1e-05
SEQ = "seq"


def shifted(block, axis, distance):
    devices = range(lax.axis_size(axis))
    route = [(i - distance, i) for i in devices if i - distance in devices]
    return lax.ppermute(block, axis, route)


def combine(earlier, later):
    return (earlier[0] * later[0], later[0][..., None, None] * earlier[1] + later[1])


def gather_level(own, axis, need_total):
    size = lax.axis_size(axis)
    place = lax.axis_index(axis)
    groups, heads = own[0].shape
    shape = own[1].shape
    tail = shape[-1]
    rows = own[1].reshape(groups, -1, tail)
    keep_rows = jnp.pad(own[0][:, None, :], ((0, 0), (0, 7), (0, tail - heads)))
    packed = jnp.concatenate([rows, keep_rows], axis=1)
    body = rows.shape[1]
    received = [None]
    for distance in range(1, size):
        if need_total:
            route = [(i, (i + distance) % size) for i in range(size)]
        else:
            route = [(i, i + distance) for i in range(size - distance)]
        got = lax.ppermute(packed, axis, route)
        received.append((got[:, body, :heads], got[:, :body].reshape(shape)))
    prefix = (jnp.ones_like(own[0]), jnp.zeros_like(own[1]))
    for distance in range(size - 1, 0, -1):
        joined = combine(prefix, received[distance])
        reach = distance <= place
        prefix = (jnp.where(reach, joined[0], prefix[0]), jnp.where(reach, joined[1], prefix[1]))
    if not need_total:
        return prefix, None
    total = combine(prefix, own)
    for distance in range(size - 1, 0, -1):
        joined = combine(total, received[distance])
        beyond = distance > place
        total = (jnp.where(beyond, joined[0], total[0]), jnp.where(beyond, joined[1], total[1]))
    return prefix, total


def entering(keep, end, axes):
    carried = (keep, end)
    prefixes = []
    for level, axis in enumerate(reversed(axes)):
        prefix, carried = gather_level(carried, axis, level < len(axes) - 1)
        prefixes.append(prefix)
    result = prefixes[-1]
    for prefix in reversed(prefixes[:-1]):
        result = combine(result, prefix)
    return result[1], prefixes[0][1]


def mix_groups(gathered, w_in, conv_w, conv_b, dt_bias, a_log, d_skip, norm_gain, after):
    groups = w_in.shape[0]
    row_count = gathered.shape[0]
    rows_first = jnp.transpose(w_in, (1, 0, 2))
    if isinstance(SEQ, tuple):
        pair = lax.axis_size(SEQ[2])
        slot = lax.axis_index(SEQ[2])
        piece = rows_first.shape[0]
        pair_w = jnp.zeros((piece * pair,) + rows_first.shape[1:], rows_first.dtype)
        for distance in range(pair):
            if distance:
                rows = lax.ppermute(
                    rows_first, SEQ[2], [(i, (i + distance) % pair) for i in range(pair)]
                )
            else:
                rows = rows_first
            source = (slot - distance) % pair
            pair_w = lax.dynamic_update_slice(pair_w, rows, (source * piece, 0, 0))
        full_w = lax.all_gather(pair_w, SEQ[:2], axis=0, tiled=True)
    else:
        full_w = lax.all_gather(rows_first, SEQ, axis=0, tiled=True)
    if after is not None:
        full_w, _ = lax.optimization_barrier((full_w, after))
    projected = jnp.einsum(
        "td,dgc->tgc",
        gathered,
        full_w,
        preferred_element_type=jnp.float32,
    )
    conv_in = projected[:, :, :CW].astype(jnp.bfloat16)
    raw_dt = projected[:, :, CW:]
    rim_rows = shifted(conv_in[row_count - (KCONV - 1) :], SEQ, 1)
    padded = jnp.concatenate([rim_rows, conv_in], axis=0)
    pre_act = jnp.broadcast_to(conv_b[None], (row_count, groups, CW))
    for offset in range(KCONV):
        pre_act = pre_act + conv_w[None, :, offset] * padded[offset : offset + row_count]
    inputs = jax.nn.silu(pre_act).astype(jnp.bfloat16)
    block_count = row_count // Q
    blocked = inputs.reshape(block_count, Q, groups, CW)
    x_all = blocked[..., :GW].reshape(block_count, Q, groups, HG, P_SIZE)
    b_all = blocked[..., GW : GW + N]
    c_all = blocked[..., GW + N :]
    step_dt = jax.nn.softplus(raw_dt + dt_bias[None]).reshape(block_count, Q, groups, HG)
    decay_rate = -jnp.exp(a_log)
    cumulative = jnp.cumsum(decay_rate[None, None] * step_dt, axis=1)
    causal = lax.broadcasted_iota(jnp.int32, (Q, Q), 0) >= lax.broadcasted_iota(
        jnp.int32, (Q, Q), 1
    )

    last_cum = cumulative[:, -1]
    keep_all = jnp.exp(last_cum)
    tail_factor = jnp.exp(last_cum[:, None] - cumulative) * step_dt
    scaled = (x_all * tail_factor[..., None]).astype(jnp.bfloat16)
    fresh_all = jnp.einsum(
        "qjghp,qjgn->qghpn", scaled, b_all, preferred_element_type=jnp.float32
    )

    local_states = []
    state_now = jnp.zeros(fresh_all.shape[1:], jnp.float32)
    keep_now = jnp.ones(keep_all.shape[1:], jnp.float32)
    keep_before = []
    for q in range(block_count):
        local_states.append(state_now)
        keep_before.append(keep_now)
        state_now = keep_all[q][..., None, None] * state_now + fresh_all[q]
        keep_now = keep_now * keep_all[q]
    incoming, first_level = entering(keep_now, state_now, SEQ if isinstance(SEQ, tuple) else (SEQ,))
    states = jnp.stack(local_states) + jnp.stack(keep_before)[..., None, None] * incoming[None]

    scores = jnp.einsum("qign,qjgn->qgij", c_all, b_all, preferred_element_type=jnp.float32)
    scores = scores + first_level.reshape(-1)[0] * 0
    cum_cols = jnp.transpose(cumulative, (0, 2, 3, 1))
    dt_cols = jnp.transpose(step_dt, (0, 2, 3, 1))
    spread = cum_cols[..., :, None] - cum_cols[..., None, :]
    damping = jnp.where(causal, jnp.exp(jnp.minimum(spread, 0.0)), 0.0)
    weights = (scores[:, :, None] * damping * dt_cols[..., None, :]).astype(jnp.bfloat16)
    partial_y = jnp.einsum(
        "qghij,qjghp->qighp", weights, x_all, preferred_element_type=jnp.float32
    )
    partial_y = partial_y + d_skip[None, None, :, :, None] * x_all

    across = jnp.einsum(
        "qign,qghpn->qighp",
        c_all,
        states.astype(jnp.bfloat16),
        preferred_element_type=jnp.float32,
    )
    activity = partial_y + jnp.exp(cumulative)[..., None] * across
    flat_act = activity.reshape(row_count, groups, GW)
    inv_rms = lax.rsqrt(jnp.mean(flat_act * flat_act, axis=-1, keepdims=True) + epsilon)
    normed = (flat_act * inv_rms * norm_gain[None]).astype(jnp.bfloat16)
    return normed.reshape(row_count, groups * GW), state_now


def per_device(tokens, w_in, conv_w, conv_b, dt_bias, a_log, d_skip, norm_gain):
    size = lax.axis_size("chan")
    place = lax.axis_index("chan")
    width = tokens.shape[1]
    gathered = jnp.zeros((tokens.shape[0], width * size), tokens.dtype)
    for distance in range(size):
        if distance:
            piece = lax.ppermute(
                tokens, "chan", [(i, (i + distance) % size) for i in range(size)]
            )
        else:
            piece = tokens
        source = (place - distance) % size
        gathered = lax.dynamic_update_slice(gathered, piece, (0, source * width))
    outputs = []
    after = None
    for g in range(w_in.shape[0]):
        one = slice(g, g + 1)
        normed, after = mix_groups(
            gathered, w_in[one], conv_w[one], conv_b[one], dt_bias[one],
            a_log[one], d_skip[one], norm_gain[one], after,
        )
        outputs.append(normed)
    return jnp.concatenate(outputs, axis=1)


def split_mesh(mesh):
    global SEQ
    devices = mesh.devices
    try:
        flat = devices.reshape(-1)
        across_y = len({d.coords[1] for d in flat})
        across_x = len({d.coords[0] for d in flat})
    except (AttributeError, IndexError, TypeError):
        SEQ = "seq"
        return mesh
    seq_size, chan_size = devices.shape
    if seq_size % (across_y * across_x) or across_y * across_x == seq_size:
        SEQ = "seq"
        return mesh
    pair = seq_size // (across_y * across_x)
    SEQ = ("y", "x", "zl")
    return Mesh(devices.reshape(across_y, across_x, pair, chan_size), SEQ + ("chan",))


def solution(mesh):
    mesh = split_mesh(mesh)
    return jax.shard_map(
        per_device,
        mesh=mesh,
        in_specs=(
            P(SEQ, "chan"),
            P("chan", SEQ, None),
            P("chan", None, None),
            P("chan", None),
            P("chan", None),
            P("chan", None),
            P("chan", None),
            P("chan", None),
        ),
        out_specs=P(SEQ, "chan"),
        check_vma=False,
    )
```

```python
import jax
import jax.numpy as jnp
from jax import lax
from jax.sharding import Mesh, PartitionSpec as P

P_SIZE = 64
N = 128
KCONV = 4
Q = 128
HG = 16
GW = 1024
CW = 1280


epsilon = 1e-05
SEQ = "seq"


def shifted(block, axis, distance):
    devices = range(lax.axis_size(axis))
    route = [(i - distance, i) for i in devices if i - distance in devices]
    return lax.ppermute(block, axis, route)


def combine(earlier, later):
    return (earlier[0] * later[0], later[0][..., None, None] * earlier[1] + later[1])


def gather_level(own, axis, need_total):
    size = lax.axis_size(axis)
    place = lax.axis_index(axis)
    groups, heads = own[0].shape
    shape = own[1].shape
    tail = shape[-1]
    rows = own[1].reshape(groups, -1, tail)
    keep_rows = jnp.pad(own[0][:, None, :], ((0, 0), (0, 7), (0, tail - heads)))
    packed = jnp.concatenate([rows, keep_rows], axis=1)
    body = rows.shape[1]
    received = [None]
    for distance in range(1, size):
        if need_total:
            route = [(i, (i + distance) % size) for i in range(size)]
        else:
            route = [(i, i + distance) for i in range(size - distance)]
        got = lax.ppermute(packed, axis, route)
        received.append((got[:, body, :heads], got[:, :body].reshape(shape)))
    prefix = (jnp.ones_like(own[0]), jnp.zeros_like(own[1]))
    for distance in range(size - 1, 0, -1):
        joined = combine(prefix, received[distance])
        reach = distance <= place
        prefix = (jnp.where(reach, joined[0], prefix[0]), jnp.where(reach, joined[1], prefix[1]))
    if not need_total:
        return prefix, None
    total = combine(prefix, own)
    for distance in range(size - 1, 0, -1):
        joined = combine(total, received[distance])
        beyond = distance > place
        total = (jnp.where(beyond, joined[0], total[0]), jnp.where(beyond, joined[1], total[1]))
    return prefix, total


def entering(keep, end, axes):
    carried = (keep, end)
    prefixes = []
    for level, axis in enumerate(reversed(axes)):
        prefix, carried = gather_level(carried, axis, level < len(axes) - 1)
        prefixes.append(prefix)
    result = prefixes[-1]
    for prefix in reversed(prefixes[:-1]):
        result = combine(result, prefix)
    return result[1]


def mix_groups(gathered, w_in, conv_w, conv_b, dt_bias, a_log, d_skip, norm_gain, after):
    groups = w_in.shape[0]
    row_count = gathered.shape[0]
    rows_first = jnp.transpose(w_in, (1, 0, 2))
    if isinstance(SEQ, tuple):
        pair = lax.axis_size(SEQ[2])
        slot = lax.axis_index(SEQ[2])
        piece = rows_first.shape[0]
        pair_w = jnp.zeros((piece * pair,) + rows_first.shape[1:], rows_first.dtype)
        for distance in range(pair):
            if distance:
                rows = lax.ppermute(
                    rows_first, SEQ[2], [(i, (i + distance) % pair) for i in range(pair)]
                )
            else:
                rows = rows_first
            source = (slot - distance) % pair
            pair_w = lax.dynamic_update_slice(pair_w, rows, (source * piece, 0, 0))
        full_w = lax.all_gather(pair_w, SEQ[:2], axis=0, tiled=True)
    else:
        full_w = lax.all_gather(rows_first, SEQ, axis=0, tiled=True)
    if after is not None:
        full_w, _ = lax.optimization_barrier((full_w, after))
    projected = jnp.einsum(
        "td,dgc->tgc",
        gathered,
        full_w,
        preferred_element_type=jnp.float32,
    )
    conv_in = projected[:, :, :CW].astype(jnp.bfloat16)
    raw_dt = projected[:, :, CW:]
    rim_rows = shifted(conv_in[row_count - (KCONV - 1) :], SEQ, 1)
    padded = jnp.concatenate([rim_rows, conv_in], axis=0)
    pre_act = jnp.broadcast_to(conv_b[None], (row_count, groups, CW))
    for offset in range(KCONV):
        pre_act = pre_act + conv_w[None, :, offset] * padded[offset : offset + row_count]
    inputs = jax.nn.silu(pre_act).astype(jnp.bfloat16)
    block_count = row_count // Q
    blocked = inputs.reshape(block_count, Q, groups, CW)
    x_all = blocked[..., :GW].reshape(block_count, Q, groups, HG, P_SIZE)
    b_all = blocked[..., GW : GW + N]
    c_all = blocked[..., GW + N :]
    step_dt = jax.nn.softplus(raw_dt + dt_bias[None]).reshape(block_count, Q, groups, HG)
    decay_rate = -jnp.exp(a_log)
    cumulative = jnp.cumsum(decay_rate[None, None] * step_dt, axis=1)
    causal = lax.broadcasted_iota(jnp.int32, (Q, Q), 0) >= lax.broadcasted_iota(
        jnp.int32, (Q, Q), 1
    )

    last_cum = cumulative[:, -1]
    keep_all = jnp.exp(last_cum)
    tail_factor = jnp.exp(last_cum[:, None] - cumulative) * step_dt
    scaled = (x_all * tail_factor[..., None]).astype(jnp.bfloat16)
    fresh_all = jnp.einsum(
        "qjghp,qjgn->qghpn", scaled, b_all, preferred_element_type=jnp.float32
    )

    local_states = []
    state_now = jnp.zeros(fresh_all.shape[1:], jnp.float32)
    keep_now = jnp.ones(keep_all.shape[1:], jnp.float32)
    keep_before = []
    for q in range(block_count):
        local_states.append(state_now)
        keep_before.append(keep_now)
        state_now = keep_all[q][..., None, None] * state_now + fresh_all[q]
        keep_now = keep_now * keep_all[q]
    incoming = entering(keep_now, state_now, SEQ if isinstance(SEQ, tuple) else (SEQ,))
    states = jnp.stack(local_states) + jnp.stack(keep_before)[..., None, None] * incoming[None]

    scores = jnp.einsum("qign,qjgn->qgij", c_all, b_all, preferred_element_type=jnp.float32)
    cum_cols = jnp.transpose(cumulative, (0, 2, 3, 1))
    dt_cols = jnp.transpose(step_dt, (0, 2, 3, 1))
    spread = cum_cols[..., :, None] - cum_cols[..., None, :]
    damping = jnp.where(causal, jnp.exp(jnp.minimum(spread, 0.0)), 0.0)
    weights = (scores[:, :, None] * damping * dt_cols[..., None, :]).astype(jnp.bfloat16)
    partial_y = jnp.einsum(
        "qghij,qjghp->qighp", weights, x_all, preferred_element_type=jnp.float32
    )

    across = jnp.einsum(
        "qign,qghpn->qighp",
        c_all,
        states.astype(jnp.bfloat16),
        preferred_element_type=jnp.float32,
    )
    activity = partial_y + jnp.exp(cumulative)[..., None] * across + d_skip[None, None, :, :, None] * x_all
    flat_act = activity.reshape(row_count, groups, GW)
    inv_rms = lax.rsqrt(jnp.mean(flat_act * flat_act, axis=-1, keepdims=True) + epsilon)
    normed = (flat_act * inv_rms * norm_gain[None]).astype(jnp.bfloat16)
    return normed.reshape(row_count, groups * GW), state_now


def per_device(tokens, w_in, conv_w, conv_b, dt_bias, a_log, d_skip, norm_gain):
    size = lax.axis_size("chan")
    place = lax.axis_index("chan")
    width = tokens.shape[1]
    gathered = jnp.zeros((tokens.shape[0], width * size), tokens.dtype)
    for distance in range(size):
        if distance:
            piece = lax.ppermute(
                tokens, "chan", [(i, (i + distance) % size) for i in range(size)]
            )
        else:
            piece = tokens
        source = (place - distance) % size
        gathered = lax.dynamic_update_slice(gathered, piece, (0, source * width))
    outputs = []
    after = None
    for g in range(w_in.shape[0]):
        one = slice(g, g + 1)
        normed, after = mix_groups(
            gathered, w_in[one], conv_w[one], conv_b[one], dt_bias[one],
            a_log[one], d_skip[one], norm_gain[one], after,
        )
        outputs.append(normed)
    return jnp.concatenate(outputs, axis=1)


def split_mesh(mesh):
    global SEQ
    devices = mesh.devices
    try:
        flat = devices.reshape(-1)
        across_y = len({d.coords[1] for d in flat})
        across_x = len({d.coords[0] for d in flat})
    except (AttributeError, IndexError, TypeError):
        SEQ = "seq"
        return mesh
    seq_size, chan_size = devices.shape
    if seq_size % (across_y * across_x) or across_y * across_x == seq_size:
        SEQ = "seq"
        return mesh
    pair = seq_size // (across_y * across_x)
    SEQ = ("y", "x", "zl")
    return Mesh(devices.reshape(across_y, across_x, pair, chan_size), SEQ + ("chan",))


def solution(mesh):
    mesh = split_mesh(mesh)
    return jax.shard_map(
        per_device,
        mesh=mesh,
        in_specs=(
            P(SEQ, "chan"),
            P("chan", SEQ, None),
            P("chan", None, None),
            P("chan", None),
            P("chan", None),
            P("chan", None),
            P("chan", None),
            P("chan", None),
        ),
        out_specs=P(SEQ, "chan"),
        check_vma=False,
    )
```

```python
import jax
import jax.numpy as jnp
from jax import lax
from jax.sharding import Mesh, PartitionSpec as P

P_SIZE = 64
N = 128
KCONV = 4
Q = 128
HG = 16
GW = 1024
CW = 1280


epsilon = 1e-05
SEQ = "seq"


def shifted(block, axis, distance):
    devices = range(lax.axis_size(axis))
    route = [(i - distance, i) for i in devices if i - distance in devices]
    return lax.ppermute(block, axis, route)


def combine(earlier, later):
    return (earlier[0] * later[0], later[0][..., None, None] * earlier[1] + later[1])


def gather_level(own, axis, need_total):
    size = lax.axis_size(axis)
    place = lax.axis_index(axis)
    groups, heads = own[0].shape
    shape = own[1].shape
    tail = shape[-1]
    rows = own[1].reshape(groups, -1, tail)
    keep_rows = jnp.pad(own[0][:, None, :], ((0, 0), (0, 7), (0, tail - heads)))
    packed = jnp.concatenate([rows, keep_rows], axis=1)
    body = rows.shape[1]
    received = [None]
    for distance in range(1, size):
        if need_total:
            route = [(i, (i + distance) % size) for i in range(size)]
        else:
            route = [(i, i + distance) for i in range(size - distance)]
        got = lax.ppermute(packed, axis, route)
        received.append((got[:, body, :heads], got[:, :body].reshape(shape)))
    prefix = (jnp.ones_like(own[0]), jnp.zeros_like(own[1]))
    for distance in range(size - 1, 0, -1):
        joined = combine(prefix, received[distance])
        reach = distance <= place
        prefix = (jnp.where(reach, joined[0], prefix[0]), jnp.where(reach, joined[1], prefix[1]))
    if not need_total:
        return prefix, None
    total = combine(prefix, own)
    for distance in range(size - 1, 0, -1):
        joined = combine(total, received[distance])
        beyond = distance > place
        total = (jnp.where(beyond, joined[0], total[0]), jnp.where(beyond, joined[1], total[1]))
    return prefix, total


def entering(keep, end, axes):
    carried = (keep, end)
    prefixes = []
    for level, axis in enumerate(reversed(axes)):
        prefix, carried = gather_level(carried, axis, level < len(axes) - 1)
        prefixes.append(prefix)
    result = prefixes[-1]
    for prefix in reversed(prefixes[:-1]):
        result = combine(result, prefix)
    return result[1]


def pair_rows(w_in):
    rows_first = jnp.transpose(w_in, (1, 0, 2))
    if not isinstance(SEQ, tuple):
        return rows_first
    pair = lax.axis_size(SEQ[2])
    slot = lax.axis_index(SEQ[2])
    piece = rows_first.shape[0]
    pair_w = jnp.zeros((piece * pair,) + rows_first.shape[1:], rows_first.dtype)
    for distance in range(pair):
        if distance:
            rows = lax.ppermute(
                rows_first, SEQ[2], [(i, (i + distance) % pair) for i in range(pair)]
            )
        else:
            rows = rows_first
        source = (slot - distance) % pair
        pair_w = lax.dynamic_update_slice(pair_w, rows, (source * piece, 0, 0))
    return pair_w


def mix_groups(gathered, pair_w, conv_w, conv_b, dt_bias, a_log, d_skip, norm_gain, after):
    groups = pair_w.shape[1]
    row_count = gathered.shape[0]
    if isinstance(SEQ, tuple):
        full_w = lax.all_gather(pair_w, SEQ[:2], axis=0, tiled=True)
    else:
        full_w = lax.all_gather(pair_w, SEQ, axis=0, tiled=True)
    if after is not None:
        full_w, _ = lax.optimization_barrier((full_w, after))
    projected = jnp.einsum(
        "td,dgc->tgc",
        gathered,
        full_w,
        preferred_element_type=jnp.float32,
    )
    conv_in = projected[:, :, :CW].astype(jnp.bfloat16)
    raw_dt = projected[:, :, CW:]
    rim_rows = shifted(conv_in[row_count - (KCONV - 1) :], SEQ, 1)
    padded = jnp.concatenate([rim_rows, conv_in], axis=0)
    pre_act = jnp.broadcast_to(conv_b[None], (row_count, groups, CW))
    for offset in range(KCONV):
        pre_act = pre_act + conv_w[None, :, offset] * padded[offset : offset + row_count]
    inputs = jax.nn.silu(pre_act).astype(jnp.bfloat16)
    block_count = row_count // Q
    blocked = inputs.reshape(block_count, Q, groups, CW)
    x_all = blocked[..., :GW].reshape(block_count, Q, groups, HG, P_SIZE)
    b_all = blocked[..., GW : GW + N]
    c_all = blocked[..., GW + N :]
    step_dt = jax.nn.softplus(raw_dt + dt_bias[None]).reshape(block_count, Q, groups, HG)
    decay_rate = -jnp.exp(a_log)
    cumulative = jnp.cumsum(decay_rate[None, None] * step_dt, axis=1)
    causal = lax.broadcasted_iota(jnp.int32, (Q, Q), 0) >= lax.broadcasted_iota(
        jnp.int32, (Q, Q), 1
    )

    last_cum = cumulative[:, -1]
    keep_all = jnp.exp(last_cum)
    tail_factor = jnp.exp(last_cum[:, None] - cumulative) * step_dt
    scaled = (x_all * tail_factor[..., None]).astype(jnp.bfloat16)
    fresh_all = jnp.einsum(
        "qjghp,qjgn->qghpn", scaled, b_all, preferred_element_type=jnp.float32
    )

    local_states = []
    state_now = jnp.zeros(fresh_all.shape[1:], jnp.float32)
    keep_now = jnp.ones(keep_all.shape[1:], jnp.float32)
    keep_before = []
    for q in range(block_count):
        local_states.append(state_now)
        keep_before.append(keep_now)
        state_now = keep_all[q][..., None, None] * state_now + fresh_all[q]
        keep_now = keep_now * keep_all[q]
    incoming = entering(keep_now, state_now, SEQ if isinstance(SEQ, tuple) else (SEQ,))
    states = jnp.stack(local_states) + jnp.stack(keep_before)[..., None, None] * incoming[None]

    scores = jnp.einsum("qign,qjgn->qgij", c_all, b_all, preferred_element_type=jnp.float32)
    cum_cols = jnp.transpose(cumulative, (0, 2, 3, 1))
    dt_cols = jnp.transpose(step_dt, (0, 2, 3, 1))
    spread = cum_cols[..., :, None] - cum_cols[..., None, :]
    damping = jnp.where(causal, jnp.exp(jnp.minimum(spread, 0.0)), 0.0)
    weights = (scores[:, :, None] * damping * dt_cols[..., None, :]).astype(jnp.bfloat16)
    partial_y = jnp.einsum(
        "qghij,qjghp->qighp", weights, x_all, preferred_element_type=jnp.float32
    )
    partial_y = partial_y + d_skip[None, None, :, :, None] * x_all

    across = jnp.einsum(
        "qign,qghpn->qighp",
        c_all,
        states.astype(jnp.bfloat16),
        preferred_element_type=jnp.float32,
    )
    activity = partial_y + jnp.exp(cumulative)[..., None] * across
    flat_act = activity.reshape(row_count, groups, GW)
    inv_rms = lax.rsqrt(jnp.mean(flat_act * flat_act, axis=-1, keepdims=True) + epsilon)
    normed = (flat_act * inv_rms * norm_gain[None]).astype(jnp.bfloat16)
    return normed.reshape(row_count, groups * GW), state_now


def per_device(tokens, w_in, conv_w, conv_b, dt_bias, a_log, d_skip, norm_gain):
    size = lax.axis_size("chan")
    place = lax.axis_index("chan")
    width = tokens.shape[1]
    gathered = jnp.zeros((tokens.shape[0], width * size), tokens.dtype)
    for distance in range(size):
        if distance:
            piece = lax.ppermute(
                tokens, "chan", [(i, (i + distance) % size) for i in range(size)]
            )
        else:
            piece = tokens
        source = (place - distance) % size
        gathered = lax.dynamic_update_slice(gathered, piece, (0, source * width))
    outputs = []
    after = None
    pair_w = pair_rows(w_in)
    for g in range(w_in.shape[0]):
        one = slice(g, g + 1)
        normed, after = mix_groups(
            gathered, pair_w[:, one], conv_w[one], conv_b[one], dt_bias[one],
            a_log[one], d_skip[one], norm_gain[one], after,
        )
        outputs.append(normed)
    return jnp.concatenate(outputs, axis=1)


def split_mesh(mesh):
    global SEQ
    devices = mesh.devices
    try:
        flat = devices.reshape(-1)
        across_y = len({d.coords[1] for d in flat})
        across_x = len({d.coords[0] for d in flat})
    except (AttributeError, IndexError, TypeError):
        SEQ = "seq"
        return mesh
    seq_size, chan_size = devices.shape
    if seq_size % (across_y * across_x) or across_y * across_x == seq_size:
        SEQ = "seq"
        return mesh
    pair = seq_size // (across_y * across_x)
    SEQ = ("y", "x", "zl")
    return Mesh(devices.reshape(across_y, across_x, pair, chan_size), SEQ + ("chan",))


def solution(mesh):
    mesh = split_mesh(mesh)
    return jax.shard_map(
        per_device,
        mesh=mesh,
        in_specs=(
            P(SEQ, "chan"),
            P("chan", SEQ, None),
            P("chan", None, None),
            P("chan", None),
            P("chan", None),
            P("chan", None),
            P("chan", None),
            P("chan", None),
        ),
        out_specs=P(SEQ, "chan"),
        check_vma=False,
    )
```

```python
import jax
import jax.numpy as jnp
from jax import lax
from jax.sharding import Mesh, PartitionSpec as P

P_SIZE = 64
N = 128
KCONV = 4
Q = 128
HG = 16
GW = 1024
CW = 1280


epsilon = 1e-05
SEQ = "seq"


def shifted(block, axis, distance):
    devices = range(lax.axis_size(axis))
    route = [(i - distance, i) for i in devices if i - distance in devices]
    return lax.ppermute(block, axis, route)


def combine(earlier, later):
    return (earlier[0] * later[0], later[0][..., None, None] * earlier[1] + later[1])


def gather_level(own, axis, need_total):
    size = lax.axis_size(axis)
    place = lax.axis_index(axis)
    groups, heads = own[0].shape
    shape = own[1].shape
    tail = shape[-1]
    rows = own[1].reshape(groups, -1, tail)
    keep_rows = jnp.pad(own[0][:, None, :], ((0, 0), (0, 7), (0, tail - heads)))
    packed = jnp.concatenate([rows, keep_rows], axis=1)
    body = rows.shape[1]
    received = [None]
    for distance in range(1, size):
        if need_total:
            route = [(i, (i + distance) % size) for i in range(size)]
        else:
            route = [(i, i + distance) for i in range(size - distance)]
        got = lax.ppermute(packed, axis, route)
        received.append((got[:, body, :heads], got[:, :body].reshape(shape)))
    prefix = (jnp.ones_like(own[0]), jnp.zeros_like(own[1]))
    for distance in range(size - 1, 0, -1):
        joined = combine(prefix, received[distance])
        reach = distance <= place
        prefix = (jnp.where(reach, joined[0], prefix[0]), jnp.where(reach, joined[1], prefix[1]))
    if not need_total:
        return prefix, None
    total = combine(prefix, own)
    for distance in range(size - 1, 0, -1):
        joined = combine(total, received[distance])
        beyond = distance > place
        total = (jnp.where(beyond, joined[0], total[0]), jnp.where(beyond, joined[1], total[1]))
    return prefix, total


def entering(keep, end, axes):
    carried = (keep, end)
    prefixes = []
    for level, axis in enumerate(reversed(axes)):
        prefix, carried = gather_level(carried, axis, level < len(axes) - 1)
        prefixes.append(prefix)
    result = prefixes[-1]
    for prefix in reversed(prefixes[:-1]):
        result = combine(result, prefix)
    return result[1]


def mix_groups(gathered, w_in, conv_w, conv_b, dt_bias, a_log, d_skip, norm_gain, after):
    groups = w_in.shape[0]
    row_count = gathered.shape[0]
    rows_first = jnp.transpose(w_in, (1, 0, 2))
    if isinstance(SEQ, tuple):
        pair = lax.axis_size(SEQ[2])
        slot = lax.axis_index(SEQ[2])
        piece = rows_first.shape[0]
        pair_w = jnp.zeros((piece * pair,) + rows_first.shape[1:], rows_first.dtype)
        for distance in range(pair):
            if distance:
                rows = lax.ppermute(
                    rows_first, SEQ[2], [(i, (i + distance) % pair) for i in range(pair)]
                )
            else:
                rows = rows_first
            source = (slot - distance) % pair
            pair_w = lax.dynamic_update_slice(pair_w, rows, (source * piece, 0, 0))
        plane_axes = SEQ[:2]
    else:
        pair_w = rows_first
        plane_axes = SEQ
    cut = GW + N
    first_w = jnp.concatenate([pair_w[..., :cut], pair_w[..., CW:]], axis=-1)
    first_w = lax.all_gather(first_w, plane_axes, axis=0, tiled=True)
    later_w = lax.all_gather(pair_w[..., cut:CW], plane_axes, axis=0, tiled=True)
    first = jnp.einsum("td,dgc->tgc", gathered, first_w, preferred_element_type=jnp.float32)
    later = jnp.einsum("td,dgc->tgc", gathered, later_w, preferred_element_type=jnp.float32)

    def convolved(part, taps, shift):
        conv_in = part.astype(jnp.bfloat16)
        rim_rows = shifted(conv_in[row_count - (KCONV - 1) :], SEQ, 1)
        padded = jnp.concatenate([rim_rows, conv_in], axis=0)
        pre_act = jnp.broadcast_to(shift[None], (row_count,) + shift.shape)
        for offset in range(KCONV):
            pre_act = pre_act + taps[None, :, offset] * padded[offset : offset + row_count]
        return jax.nn.silu(pre_act).astype(jnp.bfloat16)

    inputs_xb = convolved(first[..., :cut], conv_w[..., :cut], conv_b[..., :cut])
    raw_dt = first[..., cut:]
    inputs_c = convolved(later, conv_w[..., cut:], conv_b[..., cut:])
    block_count = row_count // Q
    blocked = inputs_xb.reshape(block_count, Q, groups, cut)
    x_all = blocked[..., :GW].reshape(block_count, Q, groups, HG, P_SIZE)
    b_all = blocked[..., GW:]
    c_all = inputs_c.reshape(block_count, Q, groups, N)
    step_dt = jax.nn.softplus(raw_dt + dt_bias[None]).reshape(block_count, Q, groups, HG)
    decay_rate = -jnp.exp(a_log)
    cumulative = jnp.cumsum(decay_rate[None, None] * step_dt, axis=1)
    causal = lax.broadcasted_iota(jnp.int32, (Q, Q), 0) >= lax.broadcasted_iota(
        jnp.int32, (Q, Q), 1
    )

    last_cum = cumulative[:, -1]
    keep_all = jnp.exp(last_cum)
    tail_factor = jnp.exp(last_cum[:, None] - cumulative) * step_dt
    scaled = (x_all * tail_factor[..., None]).astype(jnp.bfloat16)
    fresh_all = jnp.einsum(
        "qjghp,qjgn->qghpn", scaled, b_all, preferred_element_type=jnp.float32
    )

    local_states = []
    state_now = jnp.zeros(fresh_all.shape[1:], jnp.float32)
    keep_now = jnp.ones(keep_all.shape[1:], jnp.float32)
    keep_before = []
    for q in range(block_count):
        local_states.append(state_now)
        keep_before.append(keep_now)
        state_now = keep_all[q][..., None, None] * state_now + fresh_all[q]
        keep_now = keep_now * keep_all[q]
    incoming = entering(keep_now, state_now, SEQ if isinstance(SEQ, tuple) else (SEQ,))
    states = jnp.stack(local_states) + jnp.stack(keep_before)[..., None, None] * incoming[None]

    scores = jnp.einsum("qign,qjgn->qgij", c_all, b_all, preferred_element_type=jnp.float32)
    cum_cols = jnp.transpose(cumulative, (0, 2, 3, 1))
    dt_cols = jnp.transpose(step_dt, (0, 2, 3, 1))
    spread = cum_cols[..., :, None] - cum_cols[..., None, :]
    damping = jnp.where(causal, jnp.exp(jnp.minimum(spread, 0.0)), 0.0)
    weights = (scores[:, :, None] * damping * dt_cols[..., None, :]).astype(jnp.bfloat16)
    partial_y = jnp.einsum(
        "qghij,qjghp->qighp", weights, x_all, preferred_element_type=jnp.float32
    )
    partial_y = partial_y + d_skip[None, None, :, :, None] * x_all

    across = jnp.einsum(
        "qign,qghpn->qighp",
        c_all,
        states.astype(jnp.bfloat16),
        preferred_element_type=jnp.float32,
    )
    activity = partial_y + jnp.exp(cumulative)[..., None] * across
    flat_act = activity.reshape(row_count, groups, GW)
    inv_rms = lax.rsqrt(jnp.mean(flat_act * flat_act, axis=-1, keepdims=True) + epsilon)
    normed = (flat_act * inv_rms * norm_gain[None]).astype(jnp.bfloat16)
    return normed.reshape(row_count, groups * GW), state_now


def per_device(tokens, w_in, conv_w, conv_b, dt_bias, a_log, d_skip, norm_gain):
    size = lax.axis_size("chan")
    place = lax.axis_index("chan")
    width = tokens.shape[1]
    gathered = jnp.zeros((tokens.shape[0], width * size), tokens.dtype)
    for distance in range(size):
        if distance:
            piece = lax.ppermute(
                tokens, "chan", [(i, (i + distance) % size) for i in range(size)]
            )
        else:
            piece = tokens
        source = (place - distance) % size
        gathered = lax.dynamic_update_slice(gathered, piece, (0, source * width))
    normed, _ = mix_groups(
        gathered, w_in, conv_w, conv_b, dt_bias, a_log, d_skip, norm_gain, None
    )
    return normed


def split_mesh(mesh):
    global SEQ
    devices = mesh.devices
    try:
        flat = devices.reshape(-1)
        across_y = len({d.coords[1] for d in flat})
        across_x = len({d.coords[0] for d in flat})
    except (AttributeError, IndexError, TypeError):
        SEQ = "seq"
        return mesh
    seq_size, chan_size = devices.shape
    if seq_size % (across_y * across_x) or across_y * across_x == seq_size:
        SEQ = "seq"
        return mesh
    pair = seq_size // (across_y * across_x)
    SEQ = ("y", "x", "zl")
    return Mesh(devices.reshape(across_y, across_x, pair, chan_size), SEQ + ("chan",))


def solution(mesh):
    mesh = split_mesh(mesh)
    return jax.shard_map(
        per_device,
        mesh=mesh,
        in_specs=(
            P(SEQ, "chan"),
            P("chan", SEQ, None),
            P("chan", None, None),
            P("chan", None),
            P("chan", None),
            P("chan", None),
            P("chan", None),
            P("chan", None),
        ),
        out_specs=P(SEQ, "chan"),
        check_vma=False,
    )
```
